128 devices in a mesh: req: 8 (over y, core), voc: 16 (over x, z).
Axes of the slice: x: 4, y: 4, z: 4, core: 2. Of those that a mesh axis runs over, the one named last changes fastest.
Arguments:
- hidden: bfloat16 [16384, 1536], P(('req', 'voc')), may hold values from -64 to 64
- norm_gain: float32 [1536], replicated, may hold values from 0.1 to 1.9
- head: bfloat16 [1536, 49152], P(None, 'voc'), may hold values from -8 to 8
- targets: int32 [16384], P(('req', 'voc')), may hold values from 0 to 49151
- bounds: int32 [128, 2], P(('req', 'voc')), may hold values from 0 to 128, as said below
Outputs:
- logprob: float32 [16384], P(('req', 'voc'))
- entropy: float32 [16384], P(('req', 'voc'))
- target_logit: float32 [16384], P(('req', 'voc'))
- mean_entropy: float32 [1], replicated
The draws below stay inside these ranges and needn't reach their ends.
Inputs may be any that keep to these rules, and one draw needn't show every extreme that they name: bounds[d] = (lo, hi): slots lo to hi - 1 of device d hold live response rows; 1 <= hi - lo <= 96, lo <= 32; some device has hi - lo = 96 and hi = 128, some has lo = 0.
All inputs are finite; a program needn't handle non-finite values.
Results may differ from the reference program's by a relative error of at most 0.00075.
The reference program's roundings to bfloat16 on the way (of `normed`) count: a program that leaves them out, or rounds other values in their place, can miss the bound.
Values may be sent and summed in bfloat16 or wider, within the bound.
No kernel may reach another device: no remote copies, remote signals or barrier semaphores. Data moves between devices by JAX's collectives and lax.ppermute only.
A program may use at most 64 MiB of HBM per device.

```python
import math
import jax
import jax.numpy as jnp
import numpy as np
from jax import lax

D = 1536
VOCAB = 49152
ROW_DEV = 128
LIVE = 96
ROWS = 16384


def live_bounds(key):
    inner = jax.random.fold_in(key, 5)
    first_key, second_key = jax.random.split(inner)
    ndev = ROWS // ROW_DEV
    start = jax.random.randint(first_key, (ndev,), 0, ROW_DEV - LIVE + 1)
    counts = jax.random.randint(second_key, (ndev,), max(1, LIVE // 3), LIVE + 1)
    start = start.at[0].set(ROW_DEV - LIVE).at[1].set(0)
    counts = counts.at[0].set(LIVE)
    return jnp.stack([start, start + counts], axis=1).astype(jnp.int32)


def aligned_base(key):
    signs = jnp.where(jax.random.bernoulli(jax.random.fold_in(key, 77), 0.5, (8, D)), 1.0, -1.0)
    sizes = jax.random.uniform(jax.random.fold_in(key, 78), (8, D), jnp.float32, 0.8, 1.2)
    return signs * sizes * D ** (-0.5)


def row_plan(key):
    direction = jnp.clip(jax.random.normal(jax.random.fold_in(key, 11), (ROWS, D), jnp.float32), -4.0, 4.0)
    owned = jax.random.permutation(jax.random.fold_in(key, 12), VOCAB)[:ROWS].astype(jnp.int32)
    strength = 0.8 * jnp.exp(jax.random.uniform(jax.random.fold_in(key, 13), (ROWS,), jnp.float32) * math.log(10.0))
    return (direction, owned, strength)


def draw_bounds(key, part):
    return live_bounds(key)


def draw_head(key, part):
    weights = jax.random.normal(jax.random.fold_in(key, 1), (D, VOCAB), jnp.float32) * D ** (-0.5)
    weights = jnp.clip(weights, -6.0 * D ** (-0.5), 6.0 * D ** (-0.5))
    direction, owned, strength = row_plan(key)
    weights = weights.at[:, owned].set((direction * (strength[:, None] * D ** (-0.5))).T)
    base = aligned_base(key)
    level = 110.0 + jnp.arange(8, dtype=jnp.float32) * 30.0
    first = jnp.arange(8, dtype=jnp.int32) * (VOCAB // 8) + 5
    second = first + VOCAB // 16
    weights = weights.at[:, first].set((base * (level[:, None] / math.sqrt(D))).T)
    weights = weights.at[:, second].set((base * ((level[:, None] - 2.0) / math.sqrt(D))).T)
    return weights.astype(jnp.bfloat16)


def draw_hidden(key, part):
    noise = jnp.clip(jax.random.normal(jax.random.fold_in(key, 2), (ROWS, D), jnp.float32), -4.0, 4.0)
    direction, owned, strength = row_plan(key)
    values = (noise + 1.5 * direction) / 1.8
    ndev = ROWS // ROW_DEV
    bounds = live_bounds(key)
    owners = jnp.arange(8, dtype=jnp.int32) * ndev // 8
    chosen = owners * ROW_DEV + bounds[owners, 0]
    values = values.at[chosen].set(aligned_base(key) * 3.0)
    return values.astype(jnp.bfloat16)


def touch_ends(entries, key, low, top_value):
    place = [jax.random.randint(jax.random.fold_in(key, axis), (), 0, length) for axis, length in enumerate(entries.shape)]
    widest = entries.shape.index(max(entries.shape))
    neighbour = place[:widest] + [(place[widest] + 1) % entries.shape[widest]] + place[widest + 1:]
    return entries.at[tuple(place)].set(low).at[tuple(neighbour)].set(top_value)


def rank_table(number_of, skew):
    portions = [(1 << 20) // math.isqrt(grade ** skew) + 1 for grade in range(1, number_of + 1)]
    scale = 1 + sum(portions) // (1 << 30)
    return np.cumsum(np.array([max(1, weight // scale) for weight in portions]))


def ranked(own_key, extent, amount, slope):
    grid = rank_table(amount, slope)
    ticket = jax.random.randint(jax.random.fold_in(own_key, 1), extent, 0, int(grid[amount - 1]))
    rank = jnp.searchsorted(jnp.asarray(grid, jnp.int32), ticket, side="right")
    return jax.random.permutation(jax.random.fold_in(own_key, 2), amount)[rank].astype(jnp.int32)


def setup_inputs(seed: int = 0) -> dict:
    seeds = jax.random.split(jax.random.key(seed), 6)
    return {
        "hidden": draw_hidden(jax.random.fold_in(seeds[5], 71), 0),
        "norm_gain": jnp.clip(1.0 + 0.18 * jax.random.normal(seeds[1], (D,), jnp.float32), 0.1, 1.9),
        "head": draw_head(jax.random.fold_in(seeds[5], 71), 0),
        "targets": touch_ends(ranked(seeds[3], (ROWS,), VOCAB, 2), jax.random.fold_in(seeds[3], 3), 0, VOCAB - 1).astype(jnp.int32),
        "bounds": draw_bounds(jax.random.fold_in(seeds[5], 71), 0),
    }


def pick_block(count):
    size = min(count, 512)
    while count % size:
        size -= 1
    return size

def reference(hidden, norm_gain, head, targets, bounds):
    values = hidden.astype(jnp.float32)
    meansq = lax.optimization_barrier(jnp.mean(values * values, axis=-1, keepdims=True))
    normed = (values * lax.rsqrt(meansq + 1e-05) * norm_gain).astype(jnp.bfloat16)
    block = pick_block(ROWS)
    columns = jnp.arange(VOCAB, dtype=jnp.int32)

    def one_block(pair):
        rows_in, ids = pair
        logits = jnp.dot(rows_in, head, preferred_element_type=jnp.float32)
        top = lax.optimization_barrier(jnp.max(logits, axis=-1))
        expo = jnp.exp(logits - top[:, None])
        total = lax.optimization_barrier(jnp.sum(expo, axis=-1))
        weighted = lax.optimization_barrier(jnp.sum(expo * logits, axis=-1))
        picked = lax.optimization_barrier(jnp.sum(jnp.where(columns[None, :] == ids[:, None], logits, 0.0), axis=-1))
        return (top, total, weighted, picked)
    top, total, weighted, picked = lax.map(one_block, (normed.reshape(ROWS // block, block, D), targets.reshape(ROWS // block, block)))
    top, total, weighted, picked = [a.reshape(ROWS) for a in (top, total, weighted, picked)]
    lse = top + jnp.log(total)
    index = jnp.arange(ROWS, dtype=jnp.int32)
    owner = index // ROW_DEV
    slot = index % ROW_DEV
    live = (slot >= bounds[owner, 0]) & (slot < bounds[owner, 1])
    zero = jnp.zeros((ROWS,), jnp.float32)
    entropy = jnp.where(live, lse - weighted / total, zero)
    logprob = jnp.where(live, picked - lse, zero)
    target_logit = jnp.where(live, picked, zero)
    mean_entropy = (jnp.sum(entropy) / jnp.sum(live.astype(jnp.float32))).reshape(1)
    return (logprob, entropy, target_logit, mean_entropy)
```

```python
import jax
import jax.numpy as jnp
from jax import lax
from jax.sharding import PartitionSpec as P

LIVE = 96


def pick_block(count):
    size = min(count, 512)
    while count % size:
        size -= 1
    return size


def combine_stats(first, second):
    top = jnp.maximum(first[0], second[0])
    weight_a = jnp.exp(first[0] - top)
    weight_b = jnp.exp(second[0] - top)
    return jnp.stack(
        [
            top,
            first[1] * weight_a + second[1] * weight_b,
            first[2] * weight_a + second[2] * weight_b,
            first[3] + second[3],
        ]
    )


def butterfly(value, axis, combine):
    size = lax.axis_size(axis)
    index = lax.axis_index(axis)
    step = 1
    while step < size:
        other = lax.ppermute(value, axis, [(i, i ^ step) for i in range(size)])
        upper = (index & step) != 0
        first = jnp.where(upper, other, value)
        second = jnp.where(upper, value, other)
        value = combine(first, second)
        step *= 2
    return value


def shard_stats(gathered, local_ids, head):
    count = gathered.shape[0]
    width = gathered.shape[1]
    block = pick_block(count)
    columns = jnp.arange(head.shape[1], dtype=jnp.int32)

    def one_block(pair):
        rows_in, ids = pair
        logits = jnp.dot(rows_in, head, preferred_element_type=jnp.float32)
        top = jnp.max(logits, axis=-1)
        expo = jnp.exp(logits - top[:, None])
        total = jnp.sum(expo, axis=-1)
        weighted = jnp.sum(expo * logits, axis=-1)
        picked = jnp.sum(jnp.where(columns[None, :] == ids[:, None], logits, 0.0), axis=-1)
        return jnp.stack([top, total, weighted, picked])

    outputs = lax.map(
        one_block,
        (gathered.reshape(count // block, block, width), local_ids.reshape(count // block, block)),
    )
    return jnp.transpose(outputs, (1, 0, 2)).reshape(4, count)


def shards(hidden, norm_gain, head, targets, bounds):
    slots = hidden.shape[0]
    shard_width = head.shape[1]
    groups = lax.axis_size("voc")
    position = lax.axis_index("voc")
    start = bounds[0, 0]
    finish = bounds[0, 1]
    live_count = finish - start
    rows = lax.dynamic_slice_in_dim(hidden, start, LIVE, 0)
    values = rows.astype(jnp.float32)
    meansq = jnp.mean(values * values, axis=-1, keepdims=True)
    normed = (values * lax.rsqrt(meansq + 1e-05) * norm_gain).astype(jnp.bfloat16)
    ids = lax.dynamic_slice_in_dim(targets, start, LIVE, 0)
    meta = jnp.concatenate([ids, jnp.full((8,), live_count, jnp.int32)])
    gathered = lax.all_gather(normed, "voc", axis=0, tiled=True)
    gathered_meta = lax.all_gather(meta, "voc", axis=0)
    gathered_ids = gathered_meta[:, :LIVE].reshape(groups * LIVE)
    counts = gathered_meta[:, LIVE]
    local_ids = gathered_ids - position * shard_width
    stats = shard_stats(gathered, local_ids, head)
    merged = butterfly(stats, "voc", combine_stats)
    top, total, weighted, picked = merged[0], merged[1], merged[2], merged[3]
    lse = top + jnp.log(total)
    row_entropy = lse - weighted / total
    row_logprob = picked - lse
    slot = jnp.arange(LIVE, dtype=jnp.int32)
    group_live = slot[None, :] < counts[:, None]
    group_entropy = jnp.where(group_live, row_entropy.reshape(groups, LIVE), 0.0)
    totals = jnp.stack([jnp.sum(group_entropy), jnp.sum(counts).astype(jnp.float32)])
    totals = butterfly(totals, "req", lambda a, b: a + b)
    mean_entropy = (totals[0] / totals[1]).reshape(1)
    own = lambda a: lax.dynamic_slice_in_dim(a, position * LIVE, LIVE, 0)
    live = slot < live_count
    zero = jnp.zeros((LIVE,), jnp.float32)
    place = lambda a: lax.dynamic_update_slice_in_dim(jnp.zeros((slots,), jnp.float32), a, start, 0)
    entropy = place(jnp.where(live, own(row_entropy), zero))
    logprob = place(jnp.where(live, own(row_logprob), zero))
    target_logit = place(jnp.where(live, own(picked), zero))
    return (logprob, entropy, target_logit, mean_entropy)


def solution(mesh):
    placed = (
        P(("req", "voc"), None),
        P(),
        P(None, "voc"),
        P(("req", "voc")),
        P(("req", "voc"), None),
    )
    return jax.shard_map(
        shards,
        mesh=mesh,
        in_specs=placed,
        out_specs=(P(("req", "voc")), P(("req", "voc")), P(("req", "voc")), P()),
        check_vma=False,
    )
```

```python
import jax
import jax.numpy as jnp
from jax import lax
from jax.sharding import PartitionSpec as P

LIVE = 96
CHUNK = 32


def pick_block(count):
    size = min(count, 512)
    while count % size:
        size -= 1
    return size


def combine_stats(first, second):
    top = jnp.maximum(first[0], second[0])
    weight_a = jnp.exp(first[0] - top)
    weight_b = jnp.exp(second[0] - top)
    return jnp.stack(
        [
            top,
            first[1] * weight_a + second[1] * weight_b,
            first[2] * weight_a + second[2] * weight_b,
            first[3] + second[3],
        ]
    )


def butterfly(value, axis, combine):
    size = lax.axis_size(axis)
    index = lax.axis_index(axis)
    step = 1
    while step < size:
        other = lax.ppermute(value, axis, [(i, i ^ step) for i in range(size)])
        upper = (index & step) != 0
        first = jnp.where(upper, other, value)
        second = jnp.where(upper, value, other)
        value = combine(first, second)
        step *= 2
    return value


def members(value, axis, sub, stride):
    size = lax.axis_size(axis)
    digit = (lax.axis_index(axis) // stride) % sub
    received = [value]
    for shift in range(1, sub):
        pairs = []
        for i in range(size):
            d = (i // stride) % sub
            pairs.append((i, i + ((d + shift) % sub - d) * stride))
        received.append(lax.ppermute(value, axis, pairs))
    order = (digit - jnp.arange(sub, dtype=jnp.int32)) % sub
    return jnp.take(jnp.stack(received), order, axis=0)


def tree(items, combine):
    items = list(items)
    while len(items) > 1:
        items = [combine(items[i], items[i + 1]) for i in range(0, len(items), 2)]
    return items[0]


def shard_stats(gathered, local_ids, head):
    count = gathered.shape[0]
    width = gathered.shape[1]
    block = pick_block(count)
    columns = jnp.arange(head.shape[1], dtype=jnp.int32)

    def one_block(pair):
        rows_in, ids = pair
        logits = jnp.dot(rows_in, head, preferred_element_type=jnp.float32)
        top = jnp.max(logits, axis=-1)
        expo = jnp.exp(logits - top[:, None])
        total = jnp.sum(expo, axis=-1)
        weighted = jnp.sum(expo * logits, axis=-1)
        picked = jnp.sum(jnp.where(columns[None, :] == ids[:, None], logits, 0.0), axis=-1)
        return jnp.stack([top, total, weighted, picked])

    outputs = lax.map(
        one_block,
        (gathered.reshape(count // block, block, width), local_ids.reshape(count // block, block)),
    )
    return jnp.transpose(outputs, (1, 0, 2)).reshape(4, count)


def shards(hidden, norm_gain, head, targets, bounds):
    slots = hidden.shape[0]
    shard_width = head.shape[1]
    groups = lax.axis_size("voc")
    position = lax.axis_index("voc")
    start = bounds[0, 0]
    finish = bounds[0, 1]
    live_count = finish - start
    rows = lax.dynamic_slice_in_dim(hidden, start, LIVE, 0)
    values = rows.astype(jnp.float32)
    meansq = jnp.mean(values * values, axis=-1, keepdims=True)
    normed = (values * lax.rsqrt(meansq + 1e-05) * norm_gain).astype(jnp.bfloat16)
    ids = lax.dynamic_slice_in_dim(targets, start, LIVE, 0)
    meta = jnp.concatenate([ids, jnp.full((8,), live_count, jnp.int32)])
    gathered_meta = lax.all_gather(meta, "voc", axis=0)
    gathered_ids = gathered_meta[:, :LIVE]
    counts = gathered_meta[:, LIVE]
    local_ids = gathered_ids - position * shard_width
    parts = []
    for first in range(0, LIVE, CHUNK):
        gathered = lax.all_gather(normed[first:first + CHUNK], "voc", axis=0, tiled=True)
        part = shard_stats(gathered, local_ids[:, first:first + CHUNK].reshape(-1), head)
        parts.append(part.reshape(4, groups, CHUNK))
    stats = jnp.stack(parts, axis=2).reshape(4, groups * LIVE)
    inner = 4 if groups % 4 == 0 else 1
    merged = stats
    if inner > 1:
        merged = tree(members(merged, "voc", inner, 1), combine_stats)
    merged = tree(members(merged, "voc", groups // inner, inner), combine_stats)
    top, total, weighted, picked = merged[0], merged[1], merged[2], merged[3]
    lse = top + jnp.log(total)
    row_entropy = lse - weighted / total
    row_logprob = picked - lse
    slot = jnp.arange(LIVE, dtype=jnp.int32)
    group_live = slot[None, :] < counts[:, None]
    group_entropy = jnp.where(group_live, row_entropy.reshape(groups, LIVE), 0.0)
    totals = jnp.stack([jnp.sum(group_entropy), jnp.sum(counts).astype(jnp.float32)])
    totals = tree(members(totals, "req", lax.axis_size("req"), 1), lambda a, b: a + b)
    mean_entropy = (totals[0] / totals[1]).reshape(1)
    own = lambda a: lax.dynamic_slice_in_dim(a, position * LIVE, LIVE, 0)
    live = slot < live_count
    zero = jnp.zeros((LIVE,), jnp.float32)
    place = lambda a: lax.dynamic_update_slice_in_dim(jnp.zeros((slots,), jnp.float32), a, start, 0)
    entropy = place(jnp.where(live, own(row_entropy), zero))
    logprob = place(jnp.where(live, own(row_logprob), zero))
    target_logit = place(jnp.where(live, own(picked), zero))
    return (logprob, entropy, target_logit, mean_entropy)


def solution(mesh):
    placed = (
        P(("req", "voc"), None),
        P(),
        P(None, "voc"),
        P(("req", "voc")),
        P(("req", "voc"), None),
    )
    return jax.shard_map(
        shards,
        mesh=mesh,
        in_specs=placed,
        out_specs=(P(("req", "voc")), P(("req", "voc")), P(("req", "voc")), P()),
        check_vma=False,
    )
```

```python
import jax
import jax.numpy as jnp
from jax import lax
from jax.sharding import PartitionSpec as P

LIVE = 96
HALF = LIVE // 2
EXTRA = 128
SIDE = 4
AXES = ("req", "voc")


def combine_stats(first, second):
    top = jnp.maximum(first[0], second[0])
    weight_a = jnp.exp(first[0] - top)
    weight_b = jnp.exp(second[0] - top)
    return jnp.stack(
        [
            top,
            first[1] * weight_a + second[1] * weight_b,
            first[2] * weight_a + second[2] * weight_b,
            first[3] + second[3],
        ]
    )


def butterfly(value, axis, combine):
    size = lax.axis_size(axis)
    index = lax.axis_index(axis)
    step = 1
    while step < size:
        other = lax.ppermute(value, axis, [(i, i ^ step) for i in range(size)])
        upper = (index & step) != 0
        first = jnp.where(upper, other, value)
        second = jnp.where(upper, value, other)
        value = combine(first, second)
        step *= 2
    return value


def members(value, axis, sub, stride):
    size = lax.axis_size(axis)
    digit = (lax.axis_index(axis) // stride) % sub
    received = [value]
    for shift in range(1, sub):
        pairs = []
        for i in range(size):
            d = (i // stride) % sub
            pairs.append((i, i + ((d + shift) % sub - d) * stride))
        received.append(lax.ppermute(value, axis, pairs))
    order = (digit - jnp.arange(sub, dtype=jnp.int32)) % sub
    return jnp.take(jnp.stack(received), order, axis=0)


def tree(items, combine):
    items = list(items)
    while len(items) > 1:
        items = [combine(items[i], items[i + 1]) for i in range(0, len(items), 2)]
    return items[0]


def digits(voc, core):
    z, x = voc % SIDE, voc // SIDE
    return (z, x) if core == 0 else (x, z)


def compose(first, second, core):
    return first * SIDE + second if core else second * SIDE + first


def shift(value, phase, step, reqs, vocs):
    pairs = []
    for req in range(reqs):
        core = req % 2
        for voc in range(vocs):
            ring = list(digits(voc, core))
            ring[phase] = (ring[phase] + step) % SIDE
            pairs.append((req * vocs + voc, req * vocs + compose(ring[0], ring[1], core)))
    return lax.ppermute(value, AXES, pairs)


def block_stats(block, head, position):
    width = head.shape[0]
    shard_width = head.shape[1]
    rows_in = block[:, :width]
    meta = block[:, width:width + 2].astype(jnp.int32)
    ids = meta[:, 0] * 256 + meta[:, 1] - position * shard_width
    columns = jnp.arange(shard_width, dtype=jnp.int32)
    logits = jnp.dot(rows_in, head, preferred_element_type=jnp.float32)
    top = jnp.max(logits, axis=-1)
    expo = jnp.exp(logits - top[:, None])
    total = jnp.sum(expo, axis=-1)
    weighted = jnp.sum(expo * logits, axis=-1)
    picked = jnp.sum(jnp.where(columns[None, :] == ids[:, None], logits, 0.0), axis=-1)
    return jnp.stack([top, total, weighted, picked])


def shards(hidden, norm_gain, head, targets, bounds):
    slots = hidden.shape[0]
    width = hidden.shape[1]
    reqs = lax.axis_size("req")
    vocs = lax.axis_size("voc")
    position = lax.axis_index("voc")
    core = lax.axis_index("req") % 2
    start = bounds[0, 0]
    finish = bounds[0, 1]
    live_count = finish - start
    rows = lax.dynamic_slice_in_dim(hidden, start, LIVE, 0)
    values = rows.astype(jnp.float32)
    meansq = jnp.mean(values * values, axis=-1, keepdims=True)
    normed = (values * lax.rsqrt(meansq + 1e-05) * norm_gain).astype(jnp.bfloat16)
    ids = lax.dynamic_slice_in_dim(targets, start, LIVE, 0)
    meta = jnp.zeros((LIVE, EXTRA), jnp.int32)
    meta = meta.at[:, 0].set(ids // 256).at[:, 1].set(ids % 256).at[:, 2].set(live_count)
    own = jnp.concatenate([normed, meta.astype(jnp.bfloat16)], axis=1)

    stats = lambda block: block_stats(block, head, position)
    left = shift(own, 0, 1, reqs, vocs)
    right = shift(own, 0, -1, reqs, vocs)
    part_own = stats(own)
    far_a = shift(left[:HALF], 0, 1, reqs, vocs)
    far_b = shift(right[HALF:], 0, -1, reqs, vocs)
    part_near = stats(jnp.concatenate([left, right]))
    far = jnp.concatenate([far_a, far_b])
    line = jnp.stack([own, left, right, far])
    line_left = shift(line, 1, 1, reqs, vocs)
    line_right = shift(line, 1, -1, reqs, vocs)
    part_far = stats(far)
    line_far_a = shift(line_left[:, :HALF], 1, 1, reqs, vocs)
    line_far_b = shift(line_right[:, HALF:], 1, -1, reqs, vocs)
    part_lines = stats(jnp.concatenate([line_left, line_right]).reshape(-1, own.shape[1]))
    line_far = jnp.concatenate([line_far_a, line_far_b], axis=1)
    part_line_far = stats(line_far.reshape(-1, own.shape[1]))
    processed = jnp.concatenate([part_own, part_near, part_far, part_lines, part_line_far], axis=1)
    processed = processed.reshape(4, vocs, LIVE)
    blocks = jnp.concatenate(
        [own[None], left[None], right[None], far[None], line_left, line_right, line_far]
    )
    processed_counts = blocks[:, 0, width + 2].astype(jnp.int32)

    source = jnp.arange(vocs, dtype=jnp.int32)
    slot_of = jnp.array([0, 2, 3, 1], jnp.int32)
    my_a = jnp.where(core == 0, position % SIDE, position // SIDE)
    my_b = jnp.where(core == 0, position // SIDE, position % SIDE)
    src_a = jnp.where(core == 0, source % SIDE, source // SIDE)
    src_b = jnp.where(core == 0, source // SIDE, source % SIDE)
    where_is = slot_of[(src_b - my_b) % SIDE] * SIDE + slot_of[(src_a - my_a) % SIDE]
    canonical = jnp.take(processed, where_is, axis=1).reshape(4, vocs * LIVE)
    counts = jnp.take(processed_counts, where_is, axis=0)

    merged = tree(members(canonical, "voc", SIDE, 1), combine_stats)
    merged = tree(members(merged, "voc", vocs // SIDE, SIDE), combine_stats)
    top, total, weighted, picked = merged[0], merged[1], merged[2], merged[3]
    lse = top + jnp.log(total)
    row_entropy = lse - weighted / total
    row_logprob = picked - lse
    slot = jnp.arange(LIVE, dtype=jnp.int32)
    group_live = slot[None, :] < counts[:, None]
    group_entropy = jnp.where(group_live, row_entropy.reshape(vocs, LIVE), 0.0)
    totals = jnp.stack([jnp.sum(group_entropy), jnp.sum(counts).astype(jnp.float32)])
    totals = butterfly(totals, "req", lambda a, b: a + b)
    mean_entropy = (totals[0] / totals[1]).reshape(1)
    mine = lambda a: lax.dynamic_slice_in_dim(a, position * LIVE, LIVE, 0)
    live = slot < live_count
    zero = jnp.zeros((LIVE,), jnp.float32)
    place = lambda a: lax.dynamic_update_slice_in_dim(jnp.zeros((slots,), jnp.float32), a, start, 0)
    entropy = place(jnp.where(live, mine(row_entropy), zero))
    logprob = place(jnp.where(live, mine(row_logprob), zero))
    target_logit = place(jnp.where(live, mine(picked), zero))
    return (logprob, entropy, target_logit, mean_entropy)


def solution(mesh):
    placed = (
        P(AXES, None),
        P(),
        P(None, "voc"),
        P(AXES),
        P(AXES, None),
    )
    return jax.shard_map(
        shards,
        mesh=mesh,
        in_specs=placed,
        out_specs=(P(AXES), P(AXES), P(AXES), P()),
        check_vma=False,
    )
```

```python
import jax
import jax.numpy as jnp
from jax import lax
from jax.sharding import PartitionSpec as P

LIVE = 96
HALF = LIVE // 2
EXTRA = 128
SIDE = 4
AXES = ("req", "voc")


def combine_stats(first, second):
    top = jnp.maximum(first[0], second[0])
    weight_a = jnp.exp(first[0] - top)
    weight_b = jnp.exp(second[0] - top)
    return jnp.stack(
        [
            top,
            first[1] * weight_a + second[1] * weight_b,
            first[2] * weight_a + second[2] * weight_b,
            first[3] + second[3],
        ]
    )


def butterfly(value, axis, combine):
    size = lax.axis_size(axis)
    index = lax.axis_index(axis)
    step = 1
    while step < size:
        other = lax.ppermute(value, axis, [(i, i ^ step) for i in range(size)])
        upper = (index & step) != 0
        first = jnp.where(upper, other, value)
        second = jnp.where(upper, value, other)
        value = combine(first, second)
        step *= 2
    return value


def members(value, axis, sub, stride):
    size = lax.axis_size(axis)
    digit = (lax.axis_index(axis) // stride) % sub
    received = [value]
    for shift in range(1, sub):
        pairs = []
        for i in range(size):
            d = (i // stride) % sub
            pairs.append((i, i + ((d + shift) % sub - d) * stride))
        received.append(lax.ppermute(value, axis, pairs))
    order = (digit - jnp.arange(sub, dtype=jnp.int32)) % sub
    return jnp.take(jnp.stack(received), order, axis=0)


def tree(items, combine):
    items = list(items)
    while len(items) > 1:
        items = [combine(items[i], items[i + 1]) for i in range(0, len(items), 2)]
    return items[0]


def digits(voc, core):
    z, x = voc % SIDE, voc // SIDE
    return (z, x) if core == 0 else (x, z)


def compose(first, second, core):
    return first * SIDE + second if core else second * SIDE + first


def shift(value, phase, step, reqs, vocs):
    pairs = []
    for req in range(reqs):
        core = req % 2
        for voc in range(vocs):
            ring = list(digits(voc, core))
            ring[phase] = (ring[phase] + step) % SIDE
            pairs.append((req * vocs + voc, req * vocs + compose(ring[0], ring[1], core)))
    return lax.ppermute(value, AXES, pairs)


def block_stats(block, head, position):
    width = head.shape[0]
    shard_width = head.shape[1]
    rows_in = block[:, :width]
    meta = block[:, width:width + 2].astype(jnp.int32)
    ids = meta[:, 0] * 256 + meta[:, 1] - position * shard_width
    columns = jnp.arange(shard_width, dtype=jnp.int32)
    logits = jnp.dot(rows_in, head, preferred_element_type=jnp.float32)
    top = jnp.max(logits, axis=-1)
    expo = jnp.exp(logits - top[:, None])
    total = jnp.sum(expo, axis=-1)
    weighted = jnp.sum(expo * logits, axis=-1)
    picked = jnp.sum(jnp.where(columns[None, :] == ids[:, None], logits, 0.0), axis=-1)
    return jnp.stack([top, total, weighted, picked])


def shards(hidden, norm_gain, head, targets, bounds):
    slots = hidden.shape[0]
    width = hidden.shape[1]
    reqs = lax.axis_size("req")
    vocs = lax.axis_size("voc")
    position = lax.axis_index("voc")
    core = lax.axis_index("req") % 2
    start = bounds[0, 0]
    finish = bounds[0, 1]
    live_count = finish - start
    rows = lax.dynamic_slice_in_dim(hidden, start, LIVE, 0)
    values = rows.astype(jnp.float32)
    meansq = jnp.mean(values * values, axis=-1, keepdims=True)
    normed = (values * lax.rsqrt(meansq + 1e-05) * norm_gain).astype(jnp.bfloat16)
    ids = lax.dynamic_slice_in_dim(targets, start, LIVE, 0)
    meta = jnp.zeros((LIVE, EXTRA), jnp.int32)
    meta = meta.at[:, 0].set(ids // 256).at[:, 1].set(ids % 256).at[:, 2].set(live_count)
    own = jnp.concatenate([normed, meta.astype(jnp.bfloat16)], axis=1)

    stats = lambda block: block_stats(block, head, position)
    left = shift(own, 0, 1, reqs, vocs)
    right = shift(own, 0, -1, reqs, vocs)
    far_a = shift(left[:HALF], 0, 1, reqs, vocs)
    far_b = shift(right[HALF:], 0, -1, reqs, vocs)
    far = jnp.concatenate([far_a, far_b])
    line = jnp.stack([own, left, right, far])
    line_left = shift(line, 1, 1, reqs, vocs)
    line_right = shift(line, 1, -1, reqs, vocs)
    part_line = stats(line.reshape(-1, own.shape[1]))
    line_far_a = shift(line_left[:, :HALF], 1, 1, reqs, vocs)
    line_far_b = shift(line_right[:, HALF:], 1, -1, reqs, vocs)
    part_lines = stats(jnp.concatenate([line_left, line_right]).reshape(-1, own.shape[1]))
    line_far = jnp.concatenate([line_far_a, line_far_b], axis=1)
    part_line_far = stats(line_far.reshape(-1, own.shape[1]))
    processed = jnp.concatenate([part_line, part_lines, part_line_far], axis=1)
    processed = processed.reshape(4, vocs, LIVE)
    blocks = jnp.concatenate([line, line_left, line_right, line_far])
    processed_counts = blocks[:, 0, width + 2].astype(jnp.int32)

    source = jnp.arange(vocs, dtype=jnp.int32)
    slot_of = jnp.array([0, 2, 3, 1], jnp.int32)
    my_a = jnp.where(core == 0, position % SIDE, position // SIDE)
    my_b = jnp.where(core == 0, position // SIDE, position % SIDE)
    src_a = jnp.where(core == 0, source % SIDE, source // SIDE)
    src_b = jnp.where(core == 0, source // SIDE, source % SIDE)
    where_is = slot_of[(src_b - my_b) % SIDE] * SIDE + slot_of[(src_a - my_a) % SIDE]
    canonical = jnp.take(processed, where_is, axis=1).reshape(4, vocs * LIVE)
    counts = jnp.take(processed_counts, where_is, axis=0)

    merged = butterfly(canonical, "voc", combine_stats)
    top, total, weighted, picked = merged[0], merged[1], merged[2], merged[3]
    lse = top + jnp.log(total)
    row_entropy = lse - weighted / total
    row_logprob = picked - lse
    slot = jnp.arange(LIVE, dtype=jnp.int32)
    group_live = slot[None, :] < counts[:, None]
    group_entropy = jnp.where(group_live, row_entropy.reshape(vocs, LIVE), 0.0)
    totals = jnp.stack([jnp.sum(group_entropy), jnp.sum(counts).astype(jnp.float32)])
    totals = butterfly(totals, "req", lambda a, b: a + b)
    mean_entropy = (totals[0] / totals[1]).reshape(1)
    mine = lambda a: lax.dynamic_slice_in_dim(a, position * LIVE, LIVE, 0)
    live = slot < live_count
    zero = jnp.zeros((LIVE,), jnp.float32)
    place = lambda a: lax.dynamic_update_slice_in_dim(jnp.zeros((slots,), jnp.float32), a, start, 0)
    entropy = place(jnp.where(live, mine(row_entropy), zero))
    logprob = place(jnp.where(live, mine(row_logprob), zero))
    target_logit = place(jnp.where(live, mine(picked), zero))
    return (logprob, entropy, target_logit, mean_entropy)


def solution(mesh):
    placed = (
        P(AXES, None),
        P(),
        P(None, "voc"),
        P(AXES),
        P(AXES, None),
    )
    return jax.shard_map(
        shards,
        mesh=mesh,
        in_specs=placed,
        out_specs=(P(AXES), P(AXES), P(AXES), P()),
        check_vma=False,
    )
```

```python
import jax
import jax.numpy as jnp
from jax import lax
import functools
from jax.experimental import pallas as pl
from jax.experimental.pallas import tpu as pltpu
from jax.sharding import PartitionSpec as P

LIVE = 96
HALF = LIVE // 2
EXTRA = 128
SIDE = 4
AXES = ("req", "voc")
TM = 384


def combine_stats(first, second):
    top = jnp.maximum(first[0], second[0])
    weight_a = jnp.exp(first[0] - top)
    weight_b = jnp.exp(second[0] - top)
    return jnp.stack(
        [
            top,
            first[1] * weight_a + second[1] * weight_b,
            first[2] * weight_a + second[2] * weight_b,
            first[3] + second[3],
        ]
    )


def butterfly(value, axis, combine):
    size = lax.axis_size(axis)
    index = lax.axis_index(axis)
    step = 1
    while step < size:
        other = lax.ppermute(value, axis, [(i, i ^ step) for i in range(size)])
        upper = (index & step) != 0
        first = jnp.where(upper, other, value)
        second = jnp.where(upper, value, other)
        value = combine(first, second)
        step *= 2
    return value


def members(value, axis, sub, stride):
    size = lax.axis_size(axis)
    digit = (lax.axis_index(axis) // stride) % sub
    received = [value]
    for shift in range(1, sub):
        pairs = []
        for i in range(size):
            d = (i // stride) % sub
            pairs.append((i, i + ((d + shift) % sub - d) * stride))
        received.append(lax.ppermute(value, axis, pairs))
    order = (digit - jnp.arange(sub, dtype=jnp.int32)) % sub
    return jnp.take(jnp.stack(received), order, axis=0)


def tree(items, combine):
    items = list(items)
    while len(items) > 1:
        items = [combine(items[i], items[i + 1]) for i in range(0, len(items), 2)]
    return items[0]


def digits(voc, core):
    z, x = voc % SIDE, voc // SIDE
    return (z, x) if core == 0 else (x, z)


def compose(first, second, core):
    return first * SIDE + second if core else second * SIDE + first


def shift(value, phase, step, reqs, vocs):
    pairs = []
    for req in range(reqs):
        core = req % 2
        for voc in range(vocs):
            ring = list(digits(voc, core))
            ring[phase] = (ring[phase] + step) % SIDE
            pairs.append((req * vocs + voc, req * vocs + compose(ring[0], ring[1], core)))
    return lax.ppermute(value, AXES, pairs)


TN = 512

def stats_kernel(ids_ref, rows_ref, head_ref, out_ref, acc_ref, *, width):
    j = pl.program_id(1)
    @pl.when(j == 0)
    def _():
        acc_ref[0:1, :] = jnp.full((1, acc_ref.shape[1]), -jnp.inf, jnp.float32)
        acc_ref[1:4, :] = jnp.zeros((3, acc_ref.shape[1]), jnp.float32)
    rows = rows_ref[:, :width]
    s = lax.dot_general(head_ref[...], rows, (((1,), (1,)), ((), ())), preferred_element_type=jnp.float32)
    tn = s.shape[0]
    top_old = acc_ref[0:1, :]
    top = jnp.maximum(top_old, jnp.max(s, axis=0, keepdims=True))
    scale = jnp.exp(top_old - top)
    e = jnp.exp(s - top)
    total = acc_ref[1:2, :] * scale + jnp.sum(e, axis=0, keepdims=True)
    weighted = acc_ref[2:3, :] * scale + jnp.sum(e * s, axis=0, keepdims=True)
    col = lax.broadcasted_iota(jnp.int32, s.shape, 0) + j * tn
    picked = acc_ref[3:4, :] + jnp.sum(jnp.where(col == ids_ref[...], s, 0.0), axis=0, keepdims=True)
    acc_ref[0:1, :] = top
    acc_ref[1:2, :] = total
    acc_ref[2:3, :] = weighted
    acc_ref[3:4, :] = picked
    @pl.when(j == pl.num_programs(1) - 1)
    def _():
        out_ref[...] = acc_ref[...]

def pallas_stats(block, head_t, ids, tm):
    n, cols = block.shape
    vocab, width = head_t.shape
    out = pl.pallas_call(
        functools.partial(stats_kernel, width=width),
        out_shape=jax.ShapeDtypeStruct((8, n), jnp.float32),
        grid=(n // tm, vocab // TN),
        in_specs=[
            pl.BlockSpec((1, tm), lambda i, j: (0, i)),
            pl.BlockSpec((tm, cols), lambda i, j: (i, 0)),
            pl.BlockSpec((TN, width), lambda i, j: (j, 0)),
        ],
        out_specs=pl.BlockSpec((8, tm), lambda i, j: (0, i)),
        scratch_shapes=[pltpu.VMEM((8, tm), jnp.float32)],
        compiler_params=pltpu.CompilerParams(dimension_semantics=("arbitrary", "arbitrary")),
        cost_estimate=pl.CostEstimate(flops=2 * n * width * vocab, transcendentals=n * vocab,
                                      bytes_accessed=vocab * width * 2 * (n // tm) + n * cols * 2),
    )(ids.reshape(1, n), block, head_t)
    return out[:4]


def block_stats(block, head_t, position):
    width = head_t.shape[1]
    shard_width = head_t.shape[0]
    meta = block[:, width:width + 2].astype(jnp.int32)
    ids = meta[:, 0] * 256 + meta[:, 1] - position * shard_width
    return pallas_stats(block, head_t, ids, TM)


def shards(hidden, norm_gain, head, targets, bounds):
    slots = hidden.shape[0]
    width = hidden.shape[1]
    reqs = lax.axis_size("req")
    vocs = lax.axis_size("voc")
    position = lax.axis_index("voc")
    core = lax.axis_index("req") % 2
    start = bounds[0, 0]
    finish = bounds[0, 1]
    live_count = finish - start
    rows = lax.dynamic_slice_in_dim(hidden, start, LIVE, 0)
    values = rows.astype(jnp.float32)
    meansq = jnp.mean(values * values, axis=-1, keepdims=True)
    normed = (values * lax.rsqrt(meansq + 1e-05) * norm_gain).astype(jnp.bfloat16)
    ids = lax.dynamic_slice_in_dim(targets, start, LIVE, 0)
    meta = jnp.zeros((LIVE, EXTRA), jnp.int32)
    meta = meta.at[:, 0].set(ids // 256).at[:, 1].set(ids % 256).at[:, 2].set(live_count)
    own = jnp.concatenate([normed, meta.astype(jnp.bfloat16)], axis=1)

    head_t = head.T
    stats = lambda block: block_stats(block, head_t, position)
    left = shift(own, 0, 1, reqs, vocs)
    right = shift(own, 0, -1, reqs, vocs)
    far_a = shift(left[:HALF], 0, 1, reqs, vocs)
    far_b = shift(right[HALF:], 0, -1, reqs, vocs)
    far = jnp.concatenate([far_a, far_b])
    line = jnp.stack([own, left, right, far])
    line_left = shift(line, 1, 1, reqs, vocs)
    line_right = shift(line, 1, -1, reqs, vocs)
    part_line = stats(line.reshape(-1, own.shape[1]))
    part_line, line_left, line_right = lax.optimization_barrier((part_line, line_left, line_right))
    line_far_a = shift(line_left[:, :HALF], 1, 1, reqs, vocs)
    line_far_b = shift(line_right[:, HALF:], 1, -1, reqs, vocs)
    part_lines = stats(jnp.concatenate([line_left, line_right]).reshape(-1, own.shape[1]))
    part_lines, line_far_a, line_far_b = lax.optimization_barrier((part_lines, line_far_a, line_far_b))
    line_far = jnp.concatenate([line_far_a, line_far_b], axis=1)
    part_line_far = stats(line_far.reshape(-1, own.shape[1]))
    processed = jnp.concatenate([part_line, part_lines, part_line_far], axis=1)
    processed = processed.reshape(4, vocs, LIVE)
    blocks = jnp.concatenate([line, line_left, line_right, line_far])
    processed_counts = blocks[:, 0, width + 2].astype(jnp.int32)

    source = jnp.arange(vocs, dtype=jnp.int32)
    slot_of = jnp.array([0, 2, 3, 1], jnp.int32)
    my_a = jnp.where(core == 0, position % SIDE, position // SIDE)
    my_b = jnp.where(core == 0, position // SIDE, position % SIDE)
    src_a = jnp.where(core == 0, source % SIDE, source // SIDE)
    src_b = jnp.where(core == 0, source // SIDE, source % SIDE)
    where_is = slot_of[(src_b - my_b) % SIDE] * SIDE + slot_of[(src_a - my_a) % SIDE]
    canonical = jnp.take(processed, where_is, axis=1).reshape(4, vocs * LIVE)
    counts = jnp.take(processed_counts, where_is, axis=0)

    merged = butterfly(canonical, "voc", combine_stats)
    top, total, weighted, picked = merged[0], merged[1], merged[2], merged[3]
    lse = top + jnp.log(total)
    row_entropy = lse - weighted / total
    row_logprob = picked - lse
    slot = jnp.arange(LIVE, dtype=jnp.int32)
    group_live = slot[None, :] < counts[:, None]
    group_entropy = jnp.where(group_live, row_entropy.reshape(vocs, LIVE), 0.0)
    totals = jnp.stack([jnp.sum(group_entropy), jnp.sum(counts).astype(jnp.float32)])
    totals = butterfly(totals, "req", lambda a, b: a + b)
    mean_entropy = (totals[0] / totals[1]).reshape(1)
    mine = lambda a: lax.dynamic_slice_in_dim(a, position * LIVE, LIVE, 0)
    live = slot < live_count
    zero = jnp.zeros((LIVE,), jnp.float32)
    place = lambda a: lax.dynamic_update_slice_in_dim(jnp.zeros((slots,), jnp.float32), a, start, 0)
    entropy = place(jnp.where(live, mine(row_entropy), zero))
    logprob = place(jnp.where(live, mine(row_logprob), zero))
    target_logit = place(jnp.where(live, mine(picked), zero))
    return (logprob, entropy, target_logit, mean_entropy)


def solution(mesh):
    placed = (
        P(AXES, None),
        P(),
        P(None, "voc"),
        P(AXES),
        P(AXES, None),
    )
    return jax.shard_map(
        shards,
        mesh=mesh,
        in_specs=placed,
        out_specs=(P(AXES), P(AXES), P(AXES), P()),
        check_vma=False,
    )
```

```python
import jax
import jax.numpy as jnp
from jax import lax
import functools
from jax.experimental import pallas as pl
from jax.experimental.pallas import tpu as pltpu
from jax.sharding import PartitionSpec as P

LIVE = 96
HALF = LIVE // 2
EXTRA = 128
SIDE = 4
AXES = ("req", "voc")
TM = 384


def combine_stats(first, second):
    top = jnp.maximum(first[0], second[0])
    weight_a = jnp.exp(first[0] - top)
    weight_b = jnp.exp(second[0] - top)
    return jnp.stack(
        [
            top,
            first[1] * weight_a + second[1] * weight_b,
            first[2] * weight_a + second[2] * weight_b,
            first[3] + second[3],
        ]
    )


def butterfly(value, axis, combine):
    size = lax.axis_size(axis)
    index = lax.axis_index(axis)
    step = 1
    while step < size:
        other = lax.ppermute(value, axis, [(i, i ^ step) for i in range(size)])
        upper = (index & step) != 0
        first = jnp.where(upper, other, value)
        second = jnp.where(upper, value, other)
        value = combine(first, second)
        step *= 2
    return value


def members(value, axis, sub, stride):
    size = lax.axis_size(axis)
    digit = (lax.axis_index(axis) // stride) % sub
    received = [value]
    for shift in range(1, sub):
        pairs = []
        for i in range(size):
            d = (i // stride) % sub
            pairs.append((i, i + ((d + shift) % sub - d) * stride))
        received.append(lax.ppermute(value, axis, pairs))
    order = (digit - jnp.arange(sub, dtype=jnp.int32)) % sub
    return jnp.take(jnp.stack(received), order, axis=0)


def tree(items, combine):
    items = list(items)
    while len(items) > 1:
        items = [combine(items[i], items[i + 1]) for i in range(0, len(items), 2)]
    return items[0]


def digits(voc, core):
    z, x = voc % SIDE, voc // SIDE
    return (z, x) if core == 0 else (x, z)


def compose(first, second, core):
    return first * SIDE + second if core else second * SIDE + first


def shift(value, phase, step, reqs, vocs):
    pairs = []
    for req in range(reqs):
        core = req % 2
        for voc in range(vocs):
            ring = list(digits(voc, core))
            ring[phase] = (ring[phase] + step) % SIDE
            pairs.append((req * vocs + voc, req * vocs + compose(ring[0], ring[1], core)))
    return lax.ppermute(value, AXES, pairs)


TN = 512

def stats_kernel(ids_ref, rows_ref, head_ref, out_ref, acc_ref, *, width):
    j = pl.program_id(1)
    @pl.when(j == 0)
    def _():
        acc_ref[:, 0:1] = jnp.full((acc_ref.shape[0], 1), -jnp.inf, jnp.float32)
        acc_ref[:, 1:4] = jnp.zeros((acc_ref.shape[0], 3), jnp.float32)
    rows = rows_ref[:, :width]
    s = jnp.dot(rows, head_ref[...], preferred_element_type=jnp.float32)
    tn = s.shape[1]
    top_old = acc_ref[:, 0:1]
    top = jnp.maximum(top_old, jnp.max(s, axis=1, keepdims=True))
    scale = jnp.exp(top_old - top)
    e = jnp.exp(s - top)
    total = acc_ref[:, 1:2] * scale + jnp.sum(e, axis=1, keepdims=True)
    weighted = acc_ref[:, 2:3] * scale + jnp.sum(e * s, axis=1, keepdims=True)
    col = lax.broadcasted_iota(jnp.int32, s.shape, 1) + j * tn
    picked = acc_ref[:, 3:4] + jnp.sum(jnp.where(col == ids_ref[...], s, 0.0), axis=1, keepdims=True)
    acc_ref[:, 0:1] = top
    acc_ref[:, 1:2] = total
    acc_ref[:, 2:3] = weighted
    acc_ref[:, 3:4] = picked
    @pl.when(j == pl.num_programs(1) - 1)
    def _():
        out_ref[...] = acc_ref[...]

def pallas_stats(block, head, ids, tm):
    n, cols = block.shape
    width, vocab = head.shape
    out = pl.pallas_call(
        functools.partial(stats_kernel, width=width),
        out_shape=jax.ShapeDtypeStruct((n, 128), jnp.float32),
        grid=(n // tm, vocab // TN),
        in_specs=[
            pl.BlockSpec((tm, 1), lambda i, j: (i, 0)),
            pl.BlockSpec((tm, cols), lambda i, j: (i, 0)),
            pl.BlockSpec((width, TN), lambda i, j: (0, j)),
        ],
        out_specs=pl.BlockSpec((tm, 128), lambda i, j: (i, 0)),
        scratch_shapes=[pltpu.VMEM((tm, 128), jnp.float32)],
        compiler_params=pltpu.CompilerParams(dimension_semantics=("arbitrary", "arbitrary")),
        cost_estimate=pl.CostEstimate(flops=2 * n * width * vocab, transcendentals=n * vocab,
                                      bytes_accessed=vocab * width * 2 * (n // tm) + n * cols * 2),
    )(ids.reshape(n, 1), block, head)
    return out[:, :4].T


def block_stats(block, head, position):
    width = head.shape[0]
    shard_width = head.shape[1]
    meta = block[:, width:width + 2].astype(jnp.int32)
    ids = meta[:, 0] * 256 + meta[:, 1] - position * shard_width
    return pallas_stats(block, head, ids, TM)


def shards(hidden, norm_gain, head, targets, bounds):
    slots = hidden.shape[0]
    width = hidden.shape[1]
    reqs = lax.axis_size("req")
    vocs = lax.axis_size("voc")
    position = lax.axis_index("voc")
    core = lax.axis_index("req") % 2
    start = bounds[0, 0]
    finish = bounds[0, 1]
    live_count = finish - start
    rows = lax.dynamic_slice_in_dim(hidden, start, LIVE, 0)
    values = rows.astype(jnp.float32)
    meansq = jnp.mean(values * values, axis=-1, keepdims=True)
    normed = (values * lax.rsqrt(meansq + 1e-05) * norm_gain).astype(jnp.bfloat16)
    ids = lax.dynamic_slice_in_dim(targets, start, LIVE, 0)
    meta = jnp.zeros((LIVE, EXTRA), jnp.int32)
    meta = meta.at[:, 0].set(ids // 256).at[:, 1].set(ids % 256).at[:, 2].set(live_count)
    own = jnp.concatenate([normed, meta.astype(jnp.bfloat16)], axis=1)

    stats = lambda block: block_stats(block, head, position)
    left = shift(own, 0, 1, reqs, vocs)
    right = shift(own, 0, -1, reqs, vocs)
    far_a = shift(left[:HALF], 0, 1, reqs, vocs)
    far_b = shift(right[HALF:], 0, -1, reqs, vocs)
    far = jnp.concatenate([far_a, far_b])
    line = jnp.stack([own, left, right, far])
    line_left = shift(line, 1, 1, reqs, vocs)
    line_right = shift(line, 1, -1, reqs, vocs)
    part_line = stats(line.reshape(-1, own.shape[1]))
    part_line, line_left, line_right = lax.optimization_barrier((part_line, line_left, line_right))
    line_far_a = shift(line_left[:, :HALF], 1, 1, reqs, vocs)
    line_far_b = shift(line_right[:, HALF:], 1, -1, reqs, vocs)
    part_lines = stats(jnp.concatenate([line_left, line_right]).reshape(-1, own.shape[1]))
    part_lines, line_far_a, line_far_b = lax.optimization_barrier((part_lines, line_far_a, line_far_b))
    line_far = jnp.concatenate([line_far_a, line_far_b], axis=1)
    part_line_far = stats(line_far.reshape(-1, own.shape[1]))
    processed = jnp.concatenate([part_line, part_lines, part_line_far], axis=1)
    processed = processed.reshape(4, vocs, LIVE)
    blocks = jnp.concatenate([line, line_left, line_right, line_far])
    processed_counts = blocks[:, 0, width + 2].astype(jnp.int32)

    source = jnp.arange(vocs, dtype=jnp.int32)
    slot_of = jnp.array([0, 2, 3, 1], jnp.int32)
    my_a = jnp.where(core == 0, position % SIDE, position // SIDE)
    my_b = jnp.where(core == 0, position // SIDE, position % SIDE)
    src_a = jnp.where(core == 0, source % SIDE, source // SIDE)
    src_b = jnp.where(core == 0, source // SIDE, source % SIDE)
    where_is = slot_of[(src_b - my_b) % SIDE] * SIDE + slot_of[(src_a - my_a) % SIDE]
    canonical = jnp.take(processed, where_is, axis=1).reshape(4, vocs * LIVE)
    counts = jnp.take(processed_counts, where_is, axis=0)

    merged = butterfly(canonical, "voc", combine_stats)
    top, total, weighted, picked = merged[0], merged[1], merged[2], merged[3]
    lse = top + jnp.log(total)
    row_entropy = lse - weighted / total
    row_logprob = picked - lse
    slot = jnp.arange(LIVE, dtype=jnp.int32)
    group_live = slot[None, :] < counts[:, None]
    group_entropy = jnp.where(group_live, row_entropy.reshape(vocs, LIVE), 0.0)
    totals = jnp.stack([jnp.sum(group_entropy), jnp.sum(counts).astype(jnp.float32)])
    totals = butterfly(totals, "req", lambda a, b: a + b)
    mean_entropy = (totals[0] / totals[1]).reshape(1)
    mine = lambda a: lax.dynamic_slice_in_dim(a, position * LIVE, LIVE, 0)
    live = slot < live_count
    zero = jnp.zeros((LIVE,), jnp.float32)
    place = lambda a: lax.dynamic_update_slice_in_dim(jnp.zeros((slots,), jnp.float32), a, start, 0)
    entropy = place(jnp.where(live, mine(row_entropy), zero))
    logprob = place(jnp.where(live, mine(row_logprob), zero))
    target_logit = place(jnp.where(live, mine(picked), zero))
    return (logprob, entropy, target_logit, mean_entropy)


def solution(mesh):
    placed = (
        P(AXES, None),
        P(),
        P(None, "voc"),
        P(AXES),
        P(AXES, None),
    )
    return jax.shard_map(
        shards,
        mesh=mesh,
        in_specs=placed,
        out_specs=(P(AXES), P(AXES), P(AXES), P()),
        check_vma=False,
    )
```

```python
import jax
import jax.numpy as jnp
from jax import lax
from jax.sharding import PartitionSpec as P

LIVE = 96
HALF = LIVE // 2
EXTRA = 128
SIDE = 4
AXES = ("req", "voc")


def combine_stats(first, second):
    top = jnp.maximum(first[0], second[0])
    weight_a = jnp.exp(first[0] - top)
    weight_b = jnp.exp(second[0] - top)
    return jnp.stack(
        [
            top,
            first[1] * weight_a + second[1] * weight_b,
            first[2] * weight_a + second[2] * weight_b,
            first[3] + second[3],
        ]
    )


def butterfly(value, axis, combine):
    size = lax.axis_size(axis)
    index = lax.axis_index(axis)
    step = 1
    while step < size:
        other = lax.ppermute(value, axis, [(i, i ^ step) for i in range(size)])
        upper = (index & step) != 0
        first = jnp.where(upper, other, value)
        second = jnp.where(upper, value, other)
        value = combine(first, second)
        step *= 2
    return value


def members(value, axis, sub, stride):
    size = lax.axis_size(axis)
    digit = (lax.axis_index(axis) // stride) % sub
    received = [value]
    for shift in range(1, sub):
        pairs = []
        for i in range(size):
            d = (i // stride) % sub
            pairs.append((i, i + ((d + shift) % sub - d) * stride))
        received.append(lax.ppermute(value, axis, pairs))
    order = (digit - jnp.arange(sub, dtype=jnp.int32)) % sub
    return jnp.take(jnp.stack(received), order, axis=0)


def tree(items, combine):
    items = list(items)
    while len(items) > 1:
        items = [combine(items[i], items[i + 1]) for i in range(0, len(items), 2)]
    return items[0]


def digits(voc, core):
    z, x = voc % SIDE, voc // SIDE
    return (z, x) if core == 0 else (x, z)


def compose(first, second, core):
    return first * SIDE + second if core else second * SIDE + first


def shift(value, phase, step, reqs, vocs):
    pairs = []
    for req in range(reqs):
        core = req % 2
        for voc in range(vocs):
            ring = list(digits(voc, core))
            ring[phase] = (ring[phase] + step) % SIDE
            pairs.append((req * vocs + voc, req * vocs + compose(ring[0], ring[1], core)))
    return lax.ppermute(value, AXES, pairs)


def block_stats(block, head, position):
    width = head.shape[0]
    shard_width = head.shape[1]
    rows_in = block[:, :width]
    meta = block[:, width:width + 2].astype(jnp.int32)
    ids = meta[:, 0] * 256 + meta[:, 1] - position * shard_width
    columns = jnp.arange(shard_width, dtype=jnp.int32)
    logits = jnp.dot(rows_in, head, preferred_element_type=jnp.float32)
    top = jnp.max(logits, axis=-1)
    expo = jnp.exp(logits - top[:, None])
    total = jnp.sum(expo, axis=-1)
    weighted = jnp.sum(expo * logits, axis=-1)
    picked = jnp.sum(jnp.where(columns[None, :] == ids[:, None], logits, 0.0), axis=-1)
    return jnp.stack([top, total, weighted, picked])


def shards(hidden, norm_gain, head, targets, bounds):
    slots = hidden.shape[0]
    width = hidden.shape[1]
    reqs = lax.axis_size("req")
    vocs = lax.axis_size("voc")
    position = lax.axis_index("voc")
    core = lax.axis_index("req") % 2
    start = bounds[0, 0]
    finish = bounds[0, 1]
    live_count = finish - start
    rows = lax.dynamic_slice_in_dim(hidden, start, LIVE, 0)
    values = rows.astype(jnp.float32)
    meansq = jnp.mean(values * values, axis=-1, keepdims=True)
    normed = (values * lax.rsqrt(meansq + 1e-05) * norm_gain).astype(jnp.bfloat16)
    ids = lax.dynamic_slice_in_dim(targets, start, LIVE, 0)
    column = lax.broadcasted_iota(jnp.int32, (LIVE, EXTRA), 1)
    meta = jnp.where(column == 0, ids[:, None] // 256, ids[:, None] % 256)
    meta = jnp.where(column == 2, live_count, jnp.where(column < 2, meta, 0))
    own = jnp.concatenate([normed, meta.astype(jnp.bfloat16)], axis=1)

    stats = lambda block: block_stats(block, head, position)
    count_of = lambda block: block[..., :1, width + 2].reshape(-1).astype(jnp.int32)
    left = shift(own, 0, 1, reqs, vocs)
    right = shift(own, 0, -1, reqs, vocs)
    part_own = stats(own)
    part_own, left, right = lax.optimization_barrier((part_own, left, right))
    far_a = shift(left[:HALF], 0, 1, reqs, vocs)
    far_b = shift(right[HALF:], 0, -1, reqs, vocs)
    far = jnp.concatenate([far_a, far_b])
    line = jnp.stack([own, left, right, far])
    line_left = shift(line, 1, 1, reqs, vocs)
    line_right = shift(line, 1, -1, reqs, vocs)
    part_near = stats(line[1:].reshape(-1, own.shape[1]))
    part_near, line_left, line_right = lax.optimization_barrier((part_near, line_left, line_right))
    line_far_a = shift(line_left[:, :HALF], 1, 1, reqs, vocs)
    line_far_b = shift(line_right[:, HALF:], 1, -1, reqs, vocs)
    part_lines = stats(jnp.concatenate([line_left, line_right]).reshape(-1, own.shape[1]))
    part_lines, line_far_a, line_far_b = lax.optimization_barrier((part_lines, line_far_a, line_far_b))
    line_far = jnp.concatenate([line_far_a, line_far_b], axis=1)
    part_line_far = stats(line_far.reshape(-1, own.shape[1]))
    processed = jnp.concatenate([part_own, part_near, part_lines, part_line_far], axis=1)
    processed = processed.reshape(4, vocs, LIVE)
    processed_counts = jnp.concatenate(
        [count_of(line), count_of(line_left), count_of(line_right), count_of(line_far)]
    )

    source = jnp.arange(vocs, dtype=jnp.int32)
    slot_of = jnp.array([0, 2, 3, 1], jnp.int32)
    my_a = jnp.where(core == 0, position % SIDE, position // SIDE)
    my_b = jnp.where(core == 0, position // SIDE, position % SIDE)
    src_a = jnp.where(core == 0, source % SIDE, source // SIDE)
    src_b = jnp.where(core == 0, source // SIDE, source % SIDE)
    where_is = slot_of[(src_b - my_b) % SIDE] * SIDE + slot_of[(src_a - my_a) % SIDE]
    canonical = jnp.take(processed, where_is, axis=1).reshape(4, vocs * LIVE)
    counts = jnp.take(processed_counts, where_is, axis=0)

    merged = butterfly(canonical, "voc", combine_stats)
    top, total, weighted, picked = merged[0], merged[1], merged[2], merged[3]
    lse = top + jnp.log(total)
    row_entropy = lse - weighted / total
    row_logprob = picked - lse
    slot = jnp.arange(LIVE, dtype=jnp.int32)
    group_live = slot[None, :] < counts[:, None]
    group_entropy = jnp.where(group_live, row_entropy.reshape(vocs, LIVE), 0.0)
    totals = jnp.stack([jnp.sum(group_entropy), jnp.sum(counts).astype(jnp.float32)])
    totals = butterfly(totals, "req", lambda a, b: a + b)
    mean_entropy = (totals[0] / totals[1]).reshape(1)
    mine = lambda a: lax.dynamic_slice_in_dim(a, position * LIVE, LIVE, 0)
    live = slot < live_count
    zero = jnp.zeros((LIVE,), jnp.float32)
    place = lambda a: lax.dynamic_update_slice_in_dim(jnp.zeros((slots,), jnp.float32), a, start, 0)
    entropy = place(jnp.where(live, mine(row_entropy), zero))
    logprob = place(jnp.where(live, mine(row_logprob), zero))
    target_logit = place(jnp.where(live, mine(picked), zero))
    return (logprob, entropy, target_logit, mean_entropy)


def solution(mesh):
    placed = (
        P(AXES, None),
        P(),
        P(None, "voc"),
        P(AXES),
        P(AXES, None),
    )
    return jax.shard_map(
        shards,
        mesh=mesh,
        in_specs=placed,
        out_specs=(P(AXES), P(AXES), P(AXES), P()),
        check_vma=False,
    )
```

```python
import jax
import jax.numpy as jnp
from jax import lax
from jax.sharding import PartitionSpec as P

LIVE = 96
HALF = LIVE // 2
EXTRA = 128
SIDE = 4
AXES = ("req", "voc")


def combine_stats(first, second):
    top = jnp.maximum(first[0], second[0])
    weight_a = jnp.exp(first[0] - top)
    weight_b = jnp.exp(second[0] - top)
    return jnp.stack(
        [
            top,
            first[1] * weight_a + second[1] * weight_b,
            first[2] * weight_a + second[2] * weight_b,
            first[3] + second[3],
        ]
    )


def butterfly(value, axis, combine):
    size = lax.axis_size(axis)
    index = lax.axis_index(axis)
    step = 1
    while step < size:
        other = lax.ppermute(value, axis, [(i, i ^ step) for i in range(size)])
        upper = (index & step) != 0
        first = jnp.where(upper, other, value)
        second = jnp.where(upper, value, other)
        value = combine(first, second)
        step *= 2
    return value


def members(value, axis, sub, stride):
    size = lax.axis_size(axis)
    digit = (lax.axis_index(axis) // stride) % sub
    received = [value]
    for shift in range(1, sub):
        pairs = []
        for i in range(size):
            d = (i // stride) % sub
            pairs.append((i, i + ((d + shift) % sub - d) * stride))
        received.append(lax.ppermute(value, axis, pairs))
    order = (digit - jnp.arange(sub, dtype=jnp.int32)) % sub
    return jnp.take(jnp.stack(received), order, axis=0)


def tree(items, combine):
    items = list(items)
    while len(items) > 1:
        items = [combine(items[i], items[i + 1]) for i in range(0, len(items), 2)]
    return items[0]


def digits(voc, core):
    z, x = voc % SIDE, voc // SIDE
    return (z, x) if core == 0 else (x, z)


def compose(first, second, core):
    return first * SIDE + second if core else second * SIDE + first


def shift(value, phase, step, reqs, vocs):
    pairs = []
    for req in range(reqs):
        core = req % 2
        for voc in range(vocs):
            ring = list(digits(voc, core))
            ring[phase] = (ring[phase] + step) % SIDE
            pairs.append((req * vocs + voc, req * vocs + compose(ring[0], ring[1], core)))
    return lax.ppermute(value, AXES, pairs)


def block_stats(block, head, position):
    width = head.shape[0]
    shard_width = head.shape[1]
    rows_in = block[:, :width]
    meta = block[:, width:width + 2].astype(jnp.int32)
    ids = meta[:, 0] * 256 + meta[:, 1] - position * shard_width
    columns = jnp.arange(shard_width, dtype=jnp.int32)
    logits = jnp.dot(rows_in, head, preferred_element_type=jnp.float32)
    top = jnp.max(logits, axis=-1)
    expo = jnp.exp(logits - top[:, None])
    total = jnp.sum(expo, axis=-1)
    weighted = jnp.sum(expo * logits, axis=-1)
    picked = jnp.sum(jnp.where(columns[None, :] == ids[:, None], logits, 0.0), axis=-1)
    return jnp.stack([top, total, weighted, picked])


def shards(hidden, norm_gain, head, targets, bounds):
    slots = hidden.shape[0]
    width = hidden.shape[1]
    reqs = lax.axis_size("req")
    vocs = lax.axis_size("voc")
    position = lax.axis_index("voc")
    core = lax.axis_index("req") % 2
    start = bounds[0, 0]
    finish = bounds[0, 1]
    live_count = finish - start
    rows = lax.dynamic_slice_in_dim(hidden, start, LIVE, 0)
    values = rows.astype(jnp.float32)
    meansq = jnp.mean(values * values, axis=-1, keepdims=True)
    normed = (values * lax.rsqrt(meansq + 1e-05) * norm_gain).astype(jnp.bfloat16)
    ids = lax.dynamic_slice_in_dim(targets, start, LIVE, 0)
    column = lax.broadcasted_iota(jnp.int32, (LIVE, EXTRA), 1)
    meta = jnp.where(column == 0, ids[:, None] // 256, ids[:, None] % 256)
    meta = jnp.where(column == 2, live_count, jnp.where(column < 2, meta, 0))
    own = jnp.concatenate([normed, meta.astype(jnp.bfloat16)], axis=1)

    stats = lambda block: block_stats(block, head, position)
    left = shift(own, 0, 1, reqs, vocs)
    right = shift(own, 0, -1, reqs, vocs)
    part_own = stats(own)
    far_a = shift(left[:HALF], 0, 1, reqs, vocs)
    far_b = shift(right[HALF:], 0, -1, reqs, vocs)
    part_near = stats(jnp.concatenate([left, right]))
    far = jnp.concatenate([far_a, far_b])
    line = jnp.stack([own, left, right, far])
    line_left = shift(line, 1, 1, reqs, vocs)
    line_right = shift(line, 1, -1, reqs, vocs)
    part_far = stats(far)
    line_far_a = shift(line_left[:, :HALF], 1, 1, reqs, vocs)
    line_far_b = shift(line_right[:, HALF:], 1, -1, reqs, vocs)
    part_lines = stats(jnp.concatenate([line_left, line_right]).reshape(-1, own.shape[1]))
    line_far = jnp.concatenate([line_far_a, line_far_b], axis=1)
    part_line_far = stats(line_far.reshape(-1, own.shape[1]))
    processed = jnp.concatenate([part_own, part_near, part_far, part_lines, part_line_far], axis=1)
    processed = processed.reshape(4, vocs, LIVE)
    count_of = lambda block: block[..., :1, width + 2].reshape(-1).astype(jnp.int32)
    processed_counts = jnp.concatenate(
        [count_of(line), count_of(line_left), count_of(line_right), count_of(line_far)]
    )

    source = jnp.arange(vocs, dtype=jnp.int32)
    slot_of = jnp.array([0, 2, 3, 1], jnp.int32)
    my_a = jnp.where(core == 0, position % SIDE, position // SIDE)
    my_b = jnp.where(core == 0, position // SIDE, position % SIDE)
    src_a = jnp.where(core == 0, source % SIDE, source // SIDE)
    src_b = jnp.where(core == 0, source // SIDE, source % SIDE)
    where_is = slot_of[(src_b - my_b) % SIDE] * SIDE + slot_of[(src_a - my_a) % SIDE]
    canonical = jnp.take(processed, where_is, axis=1).reshape(4, vocs * LIVE)
    counts = jnp.take(processed_counts, where_is, axis=0)

    merged = butterfly(canonical, "voc", combine_stats)
    top, total, weighted, picked = merged[0], merged[1], merged[2], merged[3]
    lse = top + jnp.log(total)
    row_entropy = lse - weighted / total
    row_logprob = picked - lse
    slot = jnp.arange(LIVE, dtype=jnp.int32)
    group_live = slot[None, :] < counts[:, None]
    group_entropy = jnp.where(group_live, row_entropy.reshape(vocs, LIVE), 0.0)
    totals = jnp.stack([jnp.sum(group_entropy), jnp.sum(counts).astype(jnp.float32)])
    totals = butterfly(totals, "req", lambda a, b: a + b)
    mean_entropy = (totals[0] / totals[1]).reshape(1)
    mine = lambda a: lax.dynamic_slice_in_dim(a, position * LIVE, LIVE, 0)
    live = slot < live_count
    zero = jnp.zeros((LIVE,), jnp.float32)
    place = lambda a: lax.dynamic_update_slice_in_dim(jnp.zeros((slots,), jnp.float32), a, start, 0)
    entropy = place(jnp.where(live, mine(row_entropy), zero))
    logprob = place(jnp.where(live, mine(row_logprob), zero))
    target_logit = place(jnp.where(live, mine(picked), zero))
    return (logprob, entropy, target_logit, mean_entropy)


def solution(mesh):
    placed = (
        P(AXES, None),
        P(),
        P(None, "voc"),
        P(AXES),
        P(AXES, None),
    )
    return jax.shard_map(
        shards,
        mesh=mesh,
        in_specs=placed,
        out_specs=(P(AXES), P(AXES), P(AXES), P()),
        check_vma=False,
    )
```

```python
import jax
import jax.numpy as jnp
from jax import lax
from jax.sharding import PartitionSpec as P

LIVE = 96
HALF = LIVE // 2
EXTRA = 128
SIDE = 4
AXES = ("req", "voc")


def combine_stats(first, second):
    top = jnp.maximum(first[0], second[0])
    weight_a = jnp.exp(first[0] - top)
    weight_b = jnp.exp(second[0] - top)
    return jnp.stack(
        [
            top,
            first[1] * weight_a + second[1] * weight_b,
            first[2] * weight_a + second[2] * weight_b,
            first[3] + second[3],
        ]
    )


def butterfly(value, axis, combine):
    size = lax.axis_size(axis)
    index = lax.axis_index(axis)
    step = 1
    while step < size:
        other = lax.ppermute(value, axis, [(i, i ^ step) for i in range(size)])
        upper = (index & step) != 0
        first = jnp.where(upper, other, value)
        second = jnp.where(upper, value, other)
        value = combine(first, second)
        step *= 2
    return value


def members(value, axis, sub, stride):
    size = lax.axis_size(axis)
    digit = (lax.axis_index(axis) // stride) % sub
    received = [value]
    for shift in range(1, sub):
        pairs = []
        for i in range(size):
            d = (i // stride) % sub
            pairs.append((i, i + ((d + shift) % sub - d) * stride))
        received.append(lax.ppermute(value, axis, pairs))
    order = (digit - jnp.arange(sub, dtype=jnp.int32)) % sub
    return jnp.take(jnp.stack(received), order, axis=0)


def tree(items, combine):
    items = list(items)
    while len(items) > 1:
        items = [combine(items[i], items[i + 1]) for i in range(0, len(items), 2)]
    return items[0]


def digits(voc, core):
    z, x = voc % SIDE, voc // SIDE
    return (z, x) if core == 0 else (x, z)


def compose(first, second, core):
    return first * SIDE + second if core else second * SIDE + first


def shift(value, phase, step, reqs, vocs):
    pairs = []
    for req in range(reqs):
        core = req % 2
        for voc in range(vocs):
            ring = list(digits(voc, core))
            ring[phase] = (ring[phase] + step) % SIDE
            pairs.append((req * vocs + voc, req * vocs + compose(ring[0], ring[1], core)))
    return lax.ppermute(value, AXES, pairs)


def block_stats(block, head, position):
    width = head.shape[0]
    shard_width = head.shape[1]
    rows_in = block[:, :width]
    meta = block[:, width:width + 2].astype(jnp.int32)
    ids = meta[:, 0] * 256 + meta[:, 1] - position * shard_width
    columns = jnp.arange(shard_width, dtype=jnp.int32)
    logits = jnp.dot(rows_in, head, preferred_element_type=jnp.float32)
    top = jnp.max(logits, axis=-1)
    expo = jnp.exp(logits - top[:, None])
    total = jnp.sum(expo, axis=-1)
    weighted = jnp.sum(expo * logits, axis=-1)
    picked = jnp.sum(jnp.where(columns[None, :] == ids[:, None], logits, 0.0), axis=-1)
    return jnp.stack([top, total, weighted, picked])


def shards(hidden, norm_gain, head, targets, bounds):
    slots = hidden.shape[0]
    width = hidden.shape[1]
    reqs = lax.axis_size("req")
    vocs = lax.axis_size("voc")
    position = lax.axis_index("voc")
    core = lax.axis_index("req") % 2
    start = bounds[0, 0]
    finish = bounds[0, 1]
    live_count = finish - start
    rows = lax.dynamic_slice_in_dim(hidden, start, LIVE, 0)
    values = rows.astype(jnp.float32)
    meansq = jnp.mean(values * values, axis=-1, keepdims=True)
    normed = (values * lax.rsqrt(meansq + 1e-05) * norm_gain).astype(jnp.bfloat16)
    ids = lax.dynamic_slice_in_dim(targets, start, LIVE, 0)
    column = lax.broadcasted_iota(jnp.int32, (LIVE, EXTRA), 1)
    meta = jnp.where(column == 0, ids[:, None] // 256, ids[:, None] % 256)
    meta = jnp.where(column == 2, live_count, jnp.where(column < 2, meta, 0))
    own = jnp.concatenate([normed, meta.astype(jnp.bfloat16)], axis=1)

    stats = lambda block: block_stats(block, head, position)
    left = shift(own, 0, 1, reqs, vocs)
    right = shift(own, 0, -1, reqs, vocs)
    part_own = stats(own)
    far = shift(own, 0, 2, reqs, vocs)
    part_near = stats(jnp.concatenate([left, right]))
    line = jnp.stack([own, left, right, far])
    line_left = shift(line, 1, 1, reqs, vocs)
    line_right = shift(line, 1, -1, reqs, vocs)
    part_far = stats(far)
    line_far_a = shift(line_left[:, :HALF], 1, 1, reqs, vocs)
    line_far_b = shift(line_right[:, HALF:], 1, -1, reqs, vocs)
    part_lines = stats(jnp.concatenate([line_left, line_right]).reshape(-1, own.shape[1]))
    line_far = jnp.concatenate([line_far_a, line_far_b], axis=1)
    part_line_far = stats(line_far.reshape(-1, own.shape[1]))
    processed = jnp.concatenate([part_own, part_near, part_far, part_lines, part_line_far], axis=1)
    processed = processed.reshape(4, vocs, LIVE)
    count_of = lambda block: block[..., :1, width + 2].reshape(-1).astype(jnp.int32)
    processed_counts = jnp.concatenate(
        [count_of(line), count_of(line_left), count_of(line_right), count_of(line_far)]
    )

    source = jnp.arange(vocs, dtype=jnp.int32)
    slot_of = jnp.array([0, 2, 3, 1], jnp.int32)
    my_a = jnp.where(core == 0, position % SIDE, position // SIDE)
    my_b = jnp.where(core == 0, position // SIDE, position % SIDE)
    src_a = jnp.where(core == 0, source % SIDE, source // SIDE)
    src_b = jnp.where(core == 0, source // SIDE, source % SIDE)
    where_is = slot_of[(src_b - my_b) % SIDE] * SIDE + slot_of[(src_a - my_a) % SIDE]
    canonical = jnp.take(processed, where_is, axis=1).reshape(4, vocs * LIVE)
    counts = jnp.take(processed_counts, where_is, axis=0)

    merged = butterfly(canonical, "voc", combine_stats)
    top, total, weighted, picked = merged[0], merged[1], merged[2], merged[3]
    lse = top + jnp.log(total)
    row_entropy = lse - weighted / total
    row_logprob = picked - lse
    slot = jnp.arange(LIVE, dtype=jnp.int32)
    group_live = slot[None, :] < counts[:, None]
    group_entropy = jnp.where(group_live, row_entropy.reshape(vocs, LIVE), 0.0)
    totals = jnp.stack([jnp.sum(group_entropy), jnp.sum(counts).astype(jnp.float32)])
    totals = butterfly(totals, "req", lambda a, b: a + b)
    mean_entropy = (totals[0] / totals[1]).reshape(1)
    mine = lambda a: lax.dynamic_slice_in_dim(a, position * LIVE, LIVE, 0)
    live = slot < live_count
    zero = jnp.zeros((LIVE,), jnp.float32)
    place = lambda a: lax.dynamic_update_slice_in_dim(jnp.zeros((slots,), jnp.float32), a, start, 0)
    entropy = place(jnp.where(live, mine(row_entropy), zero))
    logprob = place(jnp.where(live, mine(row_logprob), zero))
    target_logit = place(jnp.where(live, mine(picked), zero))
    return (logprob, entropy, target_logit, mean_entropy)


def solution(mesh):
    placed = (
        P(AXES, None),
        P(),
        P(None, "voc"),
        P(AXES),
        P(AXES, None),
    )
    return jax.shard_map(
        shards,
        mesh=mesh,
        in_specs=placed,
        out_specs=(P(AXES), P(AXES), P(AXES), P()),
        check_vma=False,
    )
```

```python
import jax
import jax.numpy as jnp
from jax import lax
from jax.sharding import PartitionSpec as P

LIVE = 96
HALF = LIVE // 2
EXTRA = 128
SIDE = 4
AXES = ("req", "voc")


def combine_stats(first, second):
    top = jnp.maximum(first[0], second[0])
    weight_a = jnp.exp(first[0] - top)
    weight_b = jnp.exp(second[0] - top)
    return jnp.stack(
        [
            top,
            first[1] * weight_a + second[1] * weight_b,
            first[2] * weight_a + second[2] * weight_b,
            first[3] + second[3],
        ]
    )


def butterfly(value, axis, combine):
    size = lax.axis_size(axis)
    index = lax.axis_index(axis)
    step = 1
    while step < size:
        other = lax.ppermute(value, axis, [(i, i ^ step) for i in range(size)])
        upper = (index & step) != 0
        first = jnp.where(upper, other, value)
        second = jnp.where(upper, value, other)
        value = combine(first, second)
        step *= 2
    return value


def members(value, axis, sub, stride):
    size = lax.axis_size(axis)
    digit = (lax.axis_index(axis) // stride) % sub
    received = [value]
    for shift in range(1, sub):
        pairs = []
        for i in range(size):
            d = (i // stride) % sub
            pairs.append((i, i + ((d + shift) % sub - d) * stride))
        received.append(lax.ppermute(value, axis, pairs))
    order = (digit - jnp.arange(sub, dtype=jnp.int32)) % sub
    return jnp.take(jnp.stack(received), order, axis=0)


def tree(items, combine):
    items = list(items)
    while len(items) > 1:
        items = [combine(items[i], items[i + 1]) for i in range(0, len(items), 2)]
    return items[0]


def digits(voc, core):
    z, x = voc % SIDE, voc // SIDE
    return (z, x) if core == 0 else (x, z)


def compose(first, second, core):
    return first * SIDE + second if core else second * SIDE + first


def shift(value, phase, step, reqs, vocs):
    pairs = []
    for req in range(reqs):
        core = req % 2
        for voc in range(vocs):
            ring = list(digits(voc, core))
            ring[phase] = (ring[phase] + step) % SIDE
            pairs.append((req * vocs + voc, req * vocs + compose(ring[0], ring[1], core)))
    return lax.ppermute(value, AXES, pairs)


def block_stats(block, head, position):
    width = head.shape[0]
    shard_width = head.shape[1]
    rows_in = block[:, :width]
    meta = block[:, width:width + 2].astype(jnp.int32)
    ids = meta[:, 0] * 256 + meta[:, 1] - position * shard_width
    columns = jnp.arange(shard_width, dtype=jnp.int32)
    logits = jnp.dot(rows_in, head, preferred_element_type=jnp.float32)
    top = jnp.max(logits, axis=-1)
    expo = jnp.exp(logits - top[:, None])
    total = jnp.sum(expo, axis=-1)
    weighted = jnp.sum(expo * logits, axis=-1)
    picked = jnp.sum(jnp.where(columns[None, :] == ids[:, None], logits, 0.0), axis=-1)
    return jnp.stack([top, total, weighted, picked])


def shards(hidden, norm_gain, head, targets, bounds):
    slots = hidden.shape[0]
    width = hidden.shape[1]
    reqs = lax.axis_size("req")
    vocs = lax.axis_size("voc")
    position = lax.axis_index("voc")
    core = lax.axis_index("req") % 2
    start = bounds[0, 0]
    finish = bounds[0, 1]
    live_count = finish - start
    rows = lax.dynamic_slice_in_dim(hidden, start, LIVE, 0)
    values = rows.astype(jnp.float32)
    meansq = jnp.mean(values * values, axis=-1, keepdims=True)
    normed = (values * lax.rsqrt(meansq + 1e-05) * norm_gain).astype(jnp.bfloat16)
    ids = lax.dynamic_slice_in_dim(targets, start, LIVE, 0)
    column = lax.broadcasted_iota(jnp.int32, (LIVE, EXTRA), 1)
    meta = jnp.where(column == 0, ids[:, None] // 256, ids[:, None] % 256)
    meta = jnp.where(column == 2, live_count, jnp.where(column < 2, meta, 0))
    own = jnp.concatenate([normed, meta.astype(jnp.bfloat16)], axis=1)

    stats = lambda block: block_stats(block, head, position)
    left = shift(own, 0, 1, reqs, vocs)
    right = shift(own, 0, -1, reqs, vocs)
    part_own = stats(own)
    far = shift(own, 0, 2, reqs, vocs)
    part_near = stats(jnp.concatenate([left, right]))
    line = jnp.stack([own, left, right, far])
    line_left = shift(line, 1, 1, reqs, vocs)
    line_right = shift(line, 1, -1, reqs, vocs)
    part_far = stats(far)
    line_far = shift(line, 1, 2, reqs, vocs)
    part_line_far = stats(line_far.reshape(-1, own.shape[1]))
    part_line_far, line_left, line_right = lax.optimization_barrier((part_line_far, line_left, line_right))
    part_lines = stats(jnp.concatenate([line_left, line_right]).reshape(-1, own.shape[1]))
    processed = jnp.concatenate([part_own, part_near, part_far, part_lines, part_line_far], axis=1)
    processed = processed.reshape(4, vocs, LIVE)
    count_of = lambda block: block[..., :1, width + 2].reshape(-1).astype(jnp.int32)
    processed_counts = jnp.concatenate(
        [count_of(line), count_of(line_left), count_of(line_right), count_of(line_far)]
    )

    source = jnp.arange(vocs, dtype=jnp.int32)
    slot_of = jnp.array([0, 2, 3, 1], jnp.int32)
    my_a = jnp.where(core == 0, position % SIDE, position // SIDE)
    my_b = jnp.where(core == 0, position // SIDE, position % SIDE)
    src_a = jnp.where(core == 0, source % SIDE, source // SIDE)
    src_b = jnp.where(core == 0, source // SIDE, source % SIDE)
    where_is = slot_of[(src_b - my_b) % SIDE] * SIDE + slot_of[(src_a - my_a) % SIDE]
    canonical = jnp.take(processed, where_is, axis=1).reshape(4, vocs * LIVE)
    counts = jnp.take(processed_counts, where_is, axis=0)

    merged = butterfly(canonical, "voc", combine_stats)
    top, total, weighted, picked = merged[0], merged[1], merged[2], merged[3]
    lse = top + jnp.log(total)
    row_entropy = lse - weighted / total
    row_logprob = picked - lse
    slot = jnp.arange(LIVE, dtype=jnp.int32)
    group_live = slot[None, :] < counts[:, None]
    group_entropy = jnp.where(group_live, row_entropy.reshape(vocs, LIVE), 0.0)
    totals = jnp.stack([jnp.sum(group_entropy), jnp.sum(counts).astype(jnp.float32)])
    totals = butterfly(totals, "req", lambda a, b: a + b)
    mean_entropy = (totals[0] / totals[1]).reshape(1)
    mine = lambda a: lax.dynamic_slice_in_dim(a, position * LIVE, LIVE, 0)
    live = slot < live_count
    zero = jnp.zeros((LIVE,), jnp.float32)
    place = lambda a: lax.dynamic_update_slice_in_dim(jnp.zeros((slots,), jnp.float32), a, start, 0)
    entropy = place(jnp.where(live, mine(row_entropy), zero))
    logprob = place(jnp.where(live, mine(row_logprob), zero))
    target_logit = place(jnp.where(live, mine(picked), zero))
    return (logprob, entropy, target_logit, mean_entropy)


def solution(mesh):
    placed = (
        P(AXES, None),
        P(),
        P(None, "voc"),
        P(AXES),
        P(AXES, None),
    )
    return jax.shard_map(
        shards,
        mesh=mesh,
        in_specs=placed,
        out_specs=(P(AXES), P(AXES), P(AXES), P()),
        check_vma=False,
    )
```

```python
import jax
import jax.numpy as jnp
from jax import lax
from jax.sharding import PartitionSpec as P

LIVE = 96
HALF = LIVE // 2
EXTRA = 128
SIDE = 4
AXES = ("req", "voc")


def combine_stats(first, second):
    top = jnp.maximum(first[0], second[0])
    weight_a = jnp.exp(first[0] - top)
    weight_b = jnp.exp(second[0] - top)
    return jnp.stack(
        [
            top,
            first[1] * weight_a + second[1] * weight_b,
            first[2] * weight_a + second[2] * weight_b,
            first[3] + second[3],
        ]
    )


def butterfly(value, axis, combine):
    size = lax.axis_size(axis)
    index = lax.axis_index(axis)
    step = 1
    while step < size:
        other = lax.ppermute(value, axis, [(i, i ^ step) for i in range(size)])
        upper = (index & step) != 0
        first = jnp.where(upper, other, value)
        second = jnp.where(upper, value, other)
        value = combine(first, second)
        step *= 2
    return value


def members(value, axis, sub, stride):
    size = lax.axis_size(axis)
    digit = (lax.axis_index(axis) // stride) % sub
    received = [value]
    for shift in range(1, sub):
        pairs = []
        for i in range(size):
            d = (i // stride) % sub
            pairs.append((i, i + ((d + shift) % sub - d) * stride))
        received.append(lax.ppermute(value, axis, pairs))
    order = (digit - jnp.arange(sub, dtype=jnp.int32)) % sub
    return jnp.take(jnp.stack(received), order, axis=0)


def tree(items, combine):
    items = list(items)
    while len(items) > 1:
        items = [combine(items[i], items[i + 1]) for i in range(0, len(items), 2)]
    return items[0]


def digits(voc, core):
    z, x = voc % SIDE, voc // SIDE
    return (z, x) if core == 0 else (x, z)


def compose(first, second, core):
    return first * SIDE + second if core else second * SIDE + first


def shift(value, phase, step, reqs, vocs):
    pairs = []
    for req in range(reqs):
        core = req % 2
        for voc in range(vocs):
            ring = list(digits(voc, core))
            ring[phase] = (ring[phase] + step) % SIDE
            pairs.append((req * vocs + voc, req * vocs + compose(ring[0], ring[1], core)))
    return lax.ppermute(value, AXES, pairs)


def block_stats(block, head, position):
    width = head.shape[0]
    shard_width = head.shape[1]
    rows_in = block[:, :width]
    meta = block[:, width:width + 2].astype(jnp.int32)
    ids = meta[:, 0] * 256 + meta[:, 1] - position * shard_width
    columns = jnp.arange(shard_width, dtype=jnp.int32)
    logits = jnp.dot(rows_in, head, preferred_element_type=jnp.float32)
    top = jnp.max(logits, axis=-1)
    expo = jnp.exp(logits - top[:, None])
    total = jnp.sum(expo, axis=-1)
    weighted = jnp.sum(expo * logits, axis=-1)
    picked = jnp.sum(jnp.where(columns[None, :] == ids[:, None], logits, 0.0), axis=-1)
    return jnp.stack([top, total, weighted, picked])


def shards(hidden, norm_gain, head, targets, bounds):
    slots = hidden.shape[0]
    width = hidden.shape[1]
    reqs = lax.axis_size("req")
    vocs = lax.axis_size("voc")
    position = lax.axis_index("voc")
    core = lax.axis_index("req") % 2
    start = bounds[0, 0]
    finish = bounds[0, 1]
    live_count = finish - start
    rows = lax.dynamic_slice_in_dim(hidden, start, LIVE, 0)
    values = rows.astype(jnp.float32)
    meansq = jnp.mean(values * values, axis=-1, keepdims=True)
    normed = (values * lax.rsqrt(meansq + 1e-05) * norm_gain).astype(jnp.bfloat16)
    ids = lax.dynamic_slice_in_dim(targets, start, LIVE, 0)
    column = lax.broadcasted_iota(jnp.int32, (LIVE, EXTRA), 1)
    meta = jnp.where(column == 0, ids[:, None] // 256, ids[:, None] % 256)
    meta = jnp.where(column == 2, live_count, jnp.where(column < 2, meta, 0))
    own = jnp.concatenate([normed, meta.astype(jnp.bfloat16)], axis=1)

    stats = lambda block: block_stats(block, head, position)
    left = shift(own, 0, 1, reqs, vocs)
    right = shift(own, 0, -1, reqs, vocs)
    part_own = stats(own)
    far = shift(own, 0, 2, reqs, vocs)
    part_near = stats(jnp.concatenate([left, right]))
    line = jnp.stack([own, left, right, far])
    halves = lambda step: jnp.concatenate(
        [shift(line[:, :HALF], 1, step, reqs, vocs), shift(line[:, HALF:], 1, step, reqs, vocs)], axis=1
    )
    line_left = halves(1)
    line_right = halves(-1)
    part_far = stats(far)
    line_far = halves(2)
    part_lines = stats(jnp.concatenate([line_left, line_right]).reshape(-1, own.shape[1]))
    part_line_far = stats(line_far.reshape(-1, own.shape[1]))
    processed = jnp.concatenate([part_own, part_near, part_far, part_lines, part_line_far], axis=1)
    processed = processed.reshape(4, vocs, LIVE)
    count_of = lambda block: block[..., :1, width + 2].reshape(-1).astype(jnp.int32)
    processed_counts = jnp.concatenate(
        [count_of(line), count_of(line_left), count_of(line_right), count_of(line_far)]
    )

    source = jnp.arange(vocs, dtype=jnp.int32)
    slot_of = jnp.array([0, 2, 3, 1], jnp.int32)
    my_a = jnp.where(core == 0, position % SIDE, position // SIDE)
    my_b = jnp.where(core == 0, position // SIDE, position % SIDE)
    src_a = jnp.where(core == 0, source % SIDE, source // SIDE)
    src_b = jnp.where(core == 0, source // SIDE, source % SIDE)
    where_is = slot_of[(src_b - my_b) % SIDE] * SIDE + slot_of[(src_a - my_a) % SIDE]
    canonical = jnp.take(processed, where_is, axis=1).reshape(4, vocs * LIVE)
    counts = jnp.take(processed_counts, where_is, axis=0)

    merged = butterfly(canonical, "voc", combine_stats)
    top, total, weighted, picked = merged[0], merged[1], merged[2], merged[3]
    lse = top + jnp.log(total)
    row_entropy = lse - weighted / total
    row_logprob = picked - lse
    slot = jnp.arange(LIVE, dtype=jnp.int32)
    group_live = slot[None, :] < counts[:, None]
    group_entropy = jnp.where(group_live, row_entropy.reshape(vocs, LIVE), 0.0)
    totals = jnp.stack([jnp.sum(group_entropy), jnp.sum(counts).astype(jnp.float32)])
    totals = butterfly(totals, "req", lambda a, b: a + b)
    mean_entropy = (totals[0] / totals[1]).reshape(1)
    mine = lambda a: lax.dynamic_slice_in_dim(a, position * LIVE, LIVE, 0)
    live = slot < live_count
    zero = jnp.zeros((LIVE,), jnp.float32)
    place = lambda a: lax.dynamic_update_slice_in_dim(jnp.zeros((slots,), jnp.float32), a, start, 0)
    entropy = place(jnp.where(live, mine(row_entropy), zero))
    logprob = place(jnp.where(live, mine(row_logprob), zero))
    target_logit = place(jnp.where(live, mine(picked), zero))
    return (logprob, entropy, target_logit, mean_entropy)


def solution(mesh):
    placed = (
        P(AXES, None),
        P(),
        P(None, "voc"),
        P(AXES),
        P(AXES, None),
    )
    return jax.shard_map(
        shards,
        mesh=mesh,
        in_specs=placed,
        out_specs=(P(AXES), P(AXES), P(AXES), P()),
        check_vma=False,
    )
```

```python
import jax
import jax.numpy as jnp
from jax import lax
from jax.sharding import PartitionSpec as P

LIVE = 96
HALF = LIVE // 2
EXTRA = 128
SIDE = 4
AXES = ("req", "voc")


def combine_stats(first, second):
    top = jnp.maximum(first[0], second[0])
    weight_a = jnp.exp(first[0] - top)
    weight_b = jnp.exp(second[0] - top)
    return jnp.stack(
        [
            top,
            first[1] * weight_a + second[1] * weight_b,
            first[2] * weight_a + second[2] * weight_b,
            first[3] + second[3],
        ]
    )


def butterfly(value, axis, combine):
    size = lax.axis_size(axis)
    index = lax.axis_index(axis)
    step = 1
    while step < size:
        other = lax.ppermute(value, axis, [(i, i ^ step) for i in range(size)])
        upper = (index & step) != 0
        first = jnp.where(upper, other, value)
        second = jnp.where(upper, value, other)
        value = combine(first, second)
        step *= 2
    return value


def members(value, axis, sub, stride):
    size = lax.axis_size(axis)
    digit = (lax.axis_index(axis) // stride) % sub
    received = [value]
    for shift in range(1, sub):
        pairs = []
        for i in range(size):
            d = (i // stride) % sub
            pairs.append((i, i + ((d + shift) % sub - d) * stride))
        received.append(lax.ppermute(value, axis, pairs))
    order = (digit - jnp.arange(sub, dtype=jnp.int32)) % sub
    return jnp.take(jnp.stack(received), order, axis=0)


def tree(items, combine):
    items = list(items)
    while len(items) > 1:
        items = [combine(items[i], items[i + 1]) for i in range(0, len(items), 2)]
    return items[0]


def digits(voc, core):
    z, x = voc % SIDE, voc // SIDE
    return (z, x) if core == 0 else (x, z)


def compose(first, second, core):
    return first * SIDE + second if core else second * SIDE + first


def shift(value, phase, step, reqs, vocs):
    pairs = []
    for req in range(reqs):
        core = req % 2
        for voc in range(vocs):
            ring = list(digits(voc, core))
            ring[phase] = (ring[phase] + step) % SIDE
            pairs.append((req * vocs + voc, req * vocs + compose(ring[0], ring[1], core)))
    return lax.ppermute(value, AXES, pairs)


def block_stats(block, head, position):
    width = head.shape[0]
    shard_width = head.shape[1]
    rows_in = block[:, :width]
    meta = block[:, width:width + 2].astype(jnp.int32)
    ids = meta[:, 0] * 256 + meta[:, 1] - position * shard_width
    columns = jnp.arange(shard_width, dtype=jnp.int32)
    logits = jnp.dot(rows_in, head, preferred_element_type=jnp.float32)
    top = jnp.max(logits, axis=-1)
    expo = jnp.exp(logits - top[:, None])
    total = jnp.sum(expo, axis=-1)
    weighted = jnp.sum(expo * logits, axis=-1)
    picked = jnp.sum(jnp.where(columns[None, :] == ids[:, None], logits, 0.0), axis=-1)
    return jnp.stack([top, total, weighted, picked])


def shards(hidden, norm_gain, head, targets, bounds):
    slots = hidden.shape[0]
    width = hidden.shape[1]
    reqs = lax.axis_size("req")
    vocs = lax.axis_size("voc")
    position = lax.axis_index("voc")
    core = lax.axis_index("req") % 2
    start = bounds[0, 0]
    finish = bounds[0, 1]
    live_count = finish - start
    rows = lax.dynamic_slice_in_dim(hidden, start, LIVE, 0)
    values = rows.astype(jnp.float32)
    meansq = jnp.mean(values * values, axis=-1, keepdims=True)
    normed = (values * lax.rsqrt(meansq + 1e-05) * norm_gain).astype(jnp.bfloat16)
    ids = lax.dynamic_slice_in_dim(targets, start, LIVE, 0)
    column = lax.broadcasted_iota(jnp.int32, (LIVE, EXTRA), 1)
    meta = jnp.where(column == 0, ids[:, None] // 256, ids[:, None] % 256)
    meta = jnp.where(column == 2, live_count, jnp.where(column < 2, meta, 0))
    own = jnp.concatenate([normed, meta.astype(jnp.bfloat16)], axis=1)

    stats = lambda block: block_stats(block, head, position)
    flat = lambda blocks: blocks.reshape(-1, own.shape[1])
    left = shift(own, 0, 1, reqs, vocs)
    right = shift(own, 0, -1, reqs, vocs)
    far = shift(own, 0, 2, reqs, vocs)
    own_left = shift(own, 1, 1, reqs, vocs)
    own_right = shift(own, 1, -1, reqs, vocs)
    own_far = shift(own, 1, 2, reqs, vocs)
    part_own = stats(own)
    rest = jnp.stack([left, right, far])
    halves = lambda step: jnp.concatenate(
        [shift(rest[:, :HALF], 1, step, reqs, vocs), shift(rest[:, HALF:], 1, step, reqs, vocs)], axis=1
    )
    rest_left = halves(1)
    rest_right = halves(-1)
    rest_far = halves(2)
    early = jnp.stack([left, right, far, own_left, own_right, own_far])
    part_early = stats(flat(early))
    part_rest_far = stats(flat(rest_far))
    part_rest_sides = stats(flat(jnp.concatenate([rest_left, rest_right])))
    processed = jnp.concatenate([part_own, part_early, part_rest_sides, part_rest_far], axis=1)
    processed = processed.reshape(4, vocs, LIVE)
    count_of = lambda block: block[..., :1, width + 2].reshape(-1).astype(jnp.int32)
    processed_counts = jnp.concatenate(
        [count_of(own), count_of(early), count_of(rest_left), count_of(rest_right), count_of(rest_far)]
    )

    source = jnp.arange(vocs, dtype=jnp.int32)
    slot_of = jnp.array([0, 2, 3, 1], jnp.int32)
    my_a = jnp.where(core == 0, position % SIDE, position // SIDE)
    my_b = jnp.where(core == 0, position // SIDE, position % SIDE)
    src_a = jnp.where(core == 0, source % SIDE, source // SIDE)
    src_b = jnp.where(core == 0, source // SIDE, source % SIDE)
    order = jnp.array([[0, 1, 2, 3], [4, 7, 8, 9], [5, 10, 11, 12], [6, 13, 14, 15]], jnp.int32)
    where_is = order[slot_of[(src_b - my_b) % SIDE], slot_of[(src_a - my_a) % SIDE]]
    canonical = jnp.take(processed, where_is, axis=1).reshape(4, vocs * LIVE)
    counts = jnp.take(processed_counts, where_is, axis=0)

    merged = butterfly(canonical, "voc", combine_stats)
    top, total, weighted, picked = merged[0], merged[1], merged[2], merged[3]
    lse = top + jnp.log(total)
    row_entropy = lse - weighted / total
    row_logprob = picked - lse
    slot = jnp.arange(LIVE, dtype=jnp.int32)
    group_live = slot[None, :] < counts[:, None]
    group_entropy = jnp.where(group_live, row_entropy.reshape(vocs, LIVE), 0.0)
    totals = jnp.stack([jnp.sum(group_entropy), jnp.sum(counts).astype(jnp.float32)])
    totals = butterfly(totals, "req", lambda a, b: a + b)
    mean_entropy = (totals[0] / totals[1]).reshape(1)
    mine = lambda a: lax.dynamic_slice_in_dim(a, position * LIVE, LIVE, 0)
    live = slot < live_count
    zero = jnp.zeros((LIVE,), jnp.float32)
    place = lambda a: lax.dynamic_update_slice_in_dim(jnp.zeros((slots,), jnp.float32), a, start, 0)
    entropy = place(jnp.where(live, mine(row_entropy), zero))
    logprob = place(jnp.where(live, mine(row_logprob), zero))
    target_logit = place(jnp.where(live, mine(picked), zero))
    return (logprob, entropy, target_logit, mean_entropy)


def solution(mesh):
    placed = (
        P(AXES, None),
        P(),
        P(None, "voc"),
        P(AXES),
        P(AXES, None),
    )
    return jax.shard_map(
        shards,
        mesh=mesh,
        in_specs=placed,
        out_specs=(P(AXES), P(AXES), P(AXES), P()),
        check_vma=False,
    )
```

```python
import jax
import jax.numpy as jnp
from jax import lax
from jax.sharding import PartitionSpec as P

LIVE = 96
HALF = LIVE // 2
EXTRA = 128
SIDE = 4
AXES = ("req", "voc")


def combine_stats(first, second):
    top = jnp.maximum(first[0], second[0])
    weight_a = jnp.exp(first[0] - top)
    weight_b = jnp.exp(second[0] - top)
    return jnp.stack(
        [
            top,
            first[1] * weight_a + second[1] * weight_b,
            first[2] * weight_a + second[2] * weight_b,
            first[3] + second[3],
        ]
    )


def butterfly(value, axis, combine, flips):
    size = lax.axis_size(axis)
    index = lax.axis_index(axis)
    step = 1
    for flip in flips:
        other = lax.ppermute(value, axis, [(i, i ^ flip) for i in range(size)])
        upper = (index & step) != 0
        first = jnp.where(upper, other, value)
        second = jnp.where(upper, value, other)
        value = combine(first, second)
        step *= 2
    return value


def members(value, axis, sub, stride):
    size = lax.axis_size(axis)
    digit = (lax.axis_index(axis) // stride) % sub
    received = [value]
    for shift in range(1, sub):
        pairs = []
        for i in range(size):
            d = (i // stride) % sub
            pairs.append((i, i + ((d + shift) % sub - d) * stride))
        received.append(lax.ppermute(value, axis, pairs))
    order = (digit - jnp.arange(sub, dtype=jnp.int32)) % sub
    return jnp.take(jnp.stack(received), order, axis=0)


def tree(items, combine):
    items = list(items)
    while len(items) > 1:
        items = [combine(items[i], items[i + 1]) for i in range(0, len(items), 2)]
    return items[0]


def digits(voc, core):
    z, x = voc % SIDE, voc // SIDE
    return (z, x) if core == 0 else (x, z)


def compose(first, second, core):
    return first * SIDE + second if core else second * SIDE + first


def shift(value, phase, step, reqs, vocs):
    pairs = []
    for req in range(reqs):
        core = req % 2
        for voc in range(vocs):
            ring = list(digits(voc, core))
            ring[phase] = (ring[phase] + step) % SIDE
            pairs.append((req * vocs + voc, req * vocs + compose(ring[0], ring[1], core)))
    return lax.ppermute(value, AXES, pairs)


def block_stats(block, head, position):
    width = head.shape[0]
    shard_width = head.shape[1]
    rows_in = block[:, :width]
    meta = block[:, width:width + 2].astype(jnp.int32)
    ids = meta[:, 0] * 256 + meta[:, 1] - position * shard_width
    columns = jnp.arange(shard_width, dtype=jnp.int32)
    logits = jnp.dot(rows_in, head, preferred_element_type=jnp.float32)
    top = jnp.max(logits, axis=-1)
    expo = jnp.exp(logits - top[:, None])
    total = jnp.sum(expo, axis=-1)
    weighted = jnp.sum(expo * logits, axis=-1)
    picked = jnp.sum(jnp.where(columns[None, :] == ids[:, None], logits, 0.0), axis=-1)
    return jnp.stack([top, total, weighted, picked])


def shards(hidden, norm_gain, head, targets, bounds):
    slots = hidden.shape[0]
    width = hidden.shape[1]
    reqs = lax.axis_size("req")
    vocs = lax.axis_size("voc")
    position = lax.axis_index("voc")
    core = lax.axis_index("req") % 2
    start = bounds[0, 0]
    finish = bounds[0, 1]
    live_count = finish - start
    rows = lax.dynamic_slice_in_dim(hidden, start, LIVE, 0)
    values = rows.astype(jnp.float32)
    meansq = jnp.mean(values * values, axis=-1, keepdims=True)
    normed = (values * lax.rsqrt(meansq + 1e-05) * norm_gain).astype(jnp.bfloat16)
    ids = lax.dynamic_slice_in_dim(targets, start, LIVE, 0)
    column = lax.broadcasted_iota(jnp.int32, (LIVE, EXTRA), 1)
    meta = jnp.where(column == 0, ids[:, None] // 256, ids[:, None] % 256)
    meta = jnp.where(column == 2, live_count, jnp.where(column < 2, meta, 0))
    own = jnp.concatenate([normed, meta.astype(jnp.bfloat16)], axis=1)

    stats = lambda block: block_stats(block, head, position)
    left = shift(own, 0, 1, reqs, vocs)
    right = shift(own, 0, -1, reqs, vocs)
    part_own = stats(own)
    far = shift(own, 0, 2, reqs, vocs)
    part_near = stats(jnp.concatenate([left, right]))
    line = jnp.stack([own, left, right, far])
    halves = lambda step: jnp.concatenate(
        [shift(line[:, :HALF], 1, step, reqs, vocs), shift(line[:, HALF:], 1, step, reqs, vocs)], axis=1
    )
    line_left = halves(1)
    line_right = halves(-1)
    part_far = stats(far)
    line_far = halves(2)
    part_lines = stats(jnp.concatenate([line_left, line_right]).reshape(-1, own.shape[1]))
    part_line_far = stats(line_far.reshape(-1, own.shape[1]))
    processed = jnp.concatenate([part_own, part_near, part_far, part_lines, part_line_far], axis=1)
    processed = processed.reshape(4, vocs, LIVE)
    count_of = lambda block: block[..., :1, width + 2].reshape(-1).astype(jnp.int32)
    processed_counts = jnp.concatenate(
        [count_of(line), count_of(line_left), count_of(line_right), count_of(line_far)]
    )

    source = jnp.arange(vocs, dtype=jnp.int32)
    slot_of = jnp.array([0, 2, 3, 1], jnp.int32)
    my_a = jnp.where(core == 0, position % SIDE, position // SIDE)
    my_b = jnp.where(core == 0, position // SIDE, position % SIDE)
    src_a = jnp.where(core == 0, source % SIDE, source // SIDE)
    src_b = jnp.where(core == 0, source // SIDE, source % SIDE)
    where_is = slot_of[(src_b - my_b) % SIDE] * SIDE + slot_of[(src_a - my_a) % SIDE]
    canonical = jnp.take(processed, where_is, axis=1).reshape(4, vocs * LIVE)
    counts = jnp.take(processed_counts, where_is, axis=0)

    merged = butterfly(canonical, "voc", combine_stats, (1, 3, 4, 12))
    top, total, weighted, picked = merged[0], merged[1], merged[2], merged[3]
    lse = top + jnp.log(total)
    row_entropy = lse - weighted / total
    row_logprob = picked - lse
    slot = jnp.arange(LIVE, dtype=jnp.int32)
    group_live = slot[None, :] < counts[:, None]
    group_entropy = jnp.where(group_live, row_entropy.reshape(vocs, LIVE), 0.0)
    totals = jnp.stack([jnp.sum(group_entropy), jnp.sum(counts).astype(jnp.float32)])
    totals = butterfly(totals, "req", lambda a, b: a + b, (1, 2, 6))
    mean_entropy = (totals[0] / totals[1]).reshape(1)
    mine = lambda a: lax.dynamic_slice_in_dim(a, position * LIVE, LIVE, 0)
    live = slot < live_count
    zero = jnp.zeros((LIVE,), jnp.float32)
    place = lambda a: lax.dynamic_update_slice_in_dim(jnp.zeros((slots,), jnp.float32), a, start, 0)
    entropy = place(jnp.where(live, mine(row_entropy), zero))
    logprob = place(jnp.where(live, mine(row_logprob), zero))
    target_logit = place(jnp.where(live, mine(picked), zero))
    return (logprob, entropy, target_logit, mean_entropy)


def solution(mesh):
    placed = (
        P(AXES, None),
        P(),
        P(None, "voc"),
        P(AXES),
        P(AXES, None),
    )
    return jax.shard_map(
        shards,
        mesh=mesh,
        in_specs=placed,
        out_specs=(P(AXES), P(AXES), P(AXES), P()),
        check_vma=False,
    )
```

```python
import jax
import jax.numpy as jnp
from jax import lax
from jax.sharding import PartitionSpec as P

LIVE = 96
HALF = LIVE // 2
EXTRA = 128
SIDE = 4
AXES = ("req", "voc")


def combine_stats(first, second):
    top = jnp.maximum(first[0], second[0])
    weight_a = jnp.exp(first[0] - top)
    weight_b = jnp.exp(second[0] - top)
    return jnp.stack(
        [
            top,
            first[1] * weight_a + second[1] * weight_b,
            first[2] * weight_a + second[2] * weight_b,
            first[3] + second[3],
        ]
    )


def butterfly(value, axis, combine, flips):
    size = lax.axis_size(axis)
    index = lax.axis_index(axis)
    step = 1
    for flip in flips:
        other = lax.ppermute(value, axis, [(i, i ^ flip) for i in range(size)])
        upper = (index & step) != 0
        first = jnp.where(upper, other, value)
        second = jnp.where(upper, value, other)
        value = combine(first, second)
        step *= 2
    return value


def members(value, axis, sub, stride):
    size = lax.axis_size(axis)
    digit = (lax.axis_index(axis) // stride) % sub
    received = [value]
    for shift in range(1, sub):
        pairs = []
        for i in range(size):
            d = (i // stride) % sub
            pairs.append((i, i + ((d + shift) % sub - d) * stride))
        received.append(lax.ppermute(value, axis, pairs))
    order = (digit - jnp.arange(sub, dtype=jnp.int32)) % sub
    return jnp.take(jnp.stack(received), order, axis=0)


def tree(items, combine):
    items = list(items)
    while len(items) > 1:
        items = [combine(items[i], items[i + 1]) for i in range(0, len(items), 2)]
    return items[0]


def digits(voc, core):
    z, x = voc % SIDE, voc // SIDE
    return (z, x) if core == 0 else (x, z)


def compose(first, second, core):
    return first * SIDE + second if core else second * SIDE + first


def shift(value, phase, step, reqs, vocs):
    pairs = []
    for req in range(reqs):
        core = req % 2
        for voc in range(vocs):
            ring = list(digits(voc, core))
            ring[phase] = (ring[phase] + step) % SIDE
            pairs.append((req * vocs + voc, req * vocs + compose(ring[0], ring[1], core)))
    return lax.ppermute(value, AXES, pairs)


def block_stats(block, head, position):
    width = head.shape[0]
    shard_width = head.shape[1]
    rows_in = block[:, :width]
    meta = block[:, width:width + 2].astype(jnp.int32)
    ids = meta[:, 0] * 256 + meta[:, 1] - position * shard_width
    logits = jnp.dot(rows_in, head, preferred_element_type=jnp.float32)
    top = jnp.max(logits, axis=-1)
    expo = jnp.exp(logits - top[:, None])
    total = jnp.sum(expo, axis=-1)
    weighted = jnp.sum(expo * logits, axis=-1)
    inside = (ids >= 0) & (ids < shard_width)
    value = jnp.take_along_axis(logits, jnp.clip(ids, 0, shard_width - 1)[:, None], axis=1)[:, 0]
    picked = jnp.where(inside, value, 0.0)
    return jnp.stack([top, total, weighted, picked])


def shards(hidden, norm_gain, head, targets, bounds):
    slots = hidden.shape[0]
    width = hidden.shape[1]
    reqs = lax.axis_size("req")
    vocs = lax.axis_size("voc")
    position = lax.axis_index("voc")
    core = lax.axis_index("req") % 2
    start = bounds[0, 0]
    finish = bounds[0, 1]
    live_count = finish - start
    rows = lax.dynamic_slice_in_dim(hidden, start, LIVE, 0)
    values = rows.astype(jnp.float32)
    meansq = jnp.mean(values * values, axis=-1, keepdims=True)
    normed = (values * lax.rsqrt(meansq + 1e-05) * norm_gain).astype(jnp.bfloat16)
    ids = lax.dynamic_slice_in_dim(targets, start, LIVE, 0)
    column = lax.broadcasted_iota(jnp.int32, (LIVE, EXTRA), 1)
    meta = jnp.where(column == 0, ids[:, None] // 256, ids[:, None] % 256)
    meta = jnp.where(column == 2, live_count, jnp.where(column < 2, meta, 0))
    own = jnp.concatenate([normed, meta.astype(jnp.bfloat16)], axis=1)

    stats = lambda block: block_stats(block, head, position)
    left = shift(own, 0, 1, reqs, vocs)
    right = shift(own, 0, -1, reqs, vocs)
    part_own = stats(own)
    far = shift(own, 0, 2, reqs, vocs)
    part_near = stats(jnp.concatenate([left, right]))
    line = jnp.stack([own, left, right, far])
    halves = lambda step: jnp.concatenate(
        [shift(line[:, :HALF], 1, step, reqs, vocs), shift(line[:, HALF:], 1, step, reqs, vocs)], axis=1
    )
    line_left = halves(1)
    line_right = halves(-1)
    part_far = stats(far)
    line_far = halves(2)
    part_lines = stats(jnp.concatenate([line_left, line_right]).reshape(-1, own.shape[1]))
    part_line_far = stats(line_far.reshape(-1, own.shape[1]))
    processed = jnp.concatenate([part_own, part_near, part_far, part_lines, part_line_far], axis=1)
    processed = processed.reshape(4, vocs, LIVE)
    count_of = lambda block: block[..., :1, width + 2].reshape(-1).astype(jnp.int32)
    processed_counts = jnp.concatenate(
        [count_of(line), count_of(line_left), count_of(line_right), count_of(line_far)]
    )

    source = jnp.arange(vocs, dtype=jnp.int32)
    slot_of = jnp.array([0, 2, 3, 1], jnp.int32)
    my_a = jnp.where(core == 0, position % SIDE, position // SIDE)
    my_b = jnp.where(core == 0, position // SIDE, position % SIDE)
    src_a = jnp.where(core == 0, source % SIDE, source // SIDE)
    src_b = jnp.where(core == 0, source // SIDE, source % SIDE)
    where_is = slot_of[(src_b - my_b) % SIDE] * SIDE + slot_of[(src_a - my_a) % SIDE]
    canonical = jnp.take(processed, where_is, axis=1).reshape(4, vocs * LIVE)
    counts = jnp.take(processed_counts, where_is, axis=0)

    merged = butterfly(canonical, "voc", combine_stats, (1, 3, 4, 12))
    top, total, weighted, picked = merged[0], merged[1], merged[2], merged[3]
    lse = top + jnp.log(total)
    row_entropy = lse - weighted / total
    row_logprob = picked - lse
    slot = jnp.arange(LIVE, dtype=jnp.int32)
    group_live = slot[None, :] < counts[:, None]
    group_entropy = jnp.where(group_live, row_entropy.reshape(vocs, LIVE), 0.0)
    totals = jnp.stack([jnp.sum(group_entropy), jnp.sum(counts).astype(jnp.float32)])
    totals = butterfly(totals, "req", lambda a, b: a + b, (1, 2, 6))
    mean_entropy = (totals[0] / totals[1]).reshape(1)
    mine = lambda a: lax.dynamic_slice_in_dim(a, position * LIVE, LIVE, 0)
    live = slot < live_count
    zero = jnp.zeros((LIVE,), jnp.float32)
    place = lambda a: lax.dynamic_update_slice_in_dim(jnp.zeros((slots,), jnp.float32), a, start, 0)
    entropy = place(jnp.where(live, mine(row_entropy), zero))
    logprob = place(jnp.where(live, mine(row_logprob), zero))
    target_logit = place(jnp.where(live, mine(picked), zero))
    return (logprob, entropy, target_logit, mean_entropy)


def solution(mesh):
    placed = (
        P(AXES, None),
        P(),
        P(None, "voc"),
        P(AXES),
        P(AXES, None),
    )
    return jax.shard_map(
        shards,
        mesh=mesh,
        in_specs=placed,
        out_specs=(P(AXES), P(AXES), P(AXES), P()),
        check_vma=False,
    )
```

```python
import jax
import jax.numpy as jnp
from jax import lax
from jax.sharding import PartitionSpec as P

LIVE = 96
HALF = LIVE // 2
EXTRA = 128
SIDE = 4
AXES = ("req", "voc")


def combine_stats(first, second):
    top = jnp.maximum(first[0], second[0])
    weight_a = jnp.exp(first[0] - top)
    weight_b = jnp.exp(second[0] - top)
    return jnp.stack(
        [
            top,
            first[1] * weight_a + second[1] * weight_b,
            first[2] * weight_a + second[2] * weight_b,
            first[3] + second[3],
        ]
    )


def butterfly(value, axis, combine, flips):
    size = lax.axis_size(axis)
    index = lax.axis_index(axis)
    step = 1
    for flip in flips:
        other = lax.ppermute(value, axis, [(i, i ^ flip) for i in range(size)])
        upper = (index & step) != 0
        first = jnp.where(upper, other, value)
        second = jnp.where(upper, value, other)
        value = combine(first, second)
        step *= 2
    return value


def members(value, axis, sub, stride):
    size = lax.axis_size(axis)
    digit = (lax.axis_index(axis) // stride) % sub
    received = [value]
    for shift in range(1, sub):
        pairs = []
        for i in range(size):
            d = (i // stride) % sub
            pairs.append((i, i + ((d + shift) % sub - d) * stride))
        received.append(lax.ppermute(value, axis, pairs))
    order = (digit - jnp.arange(sub, dtype=jnp.int32)) % sub
    return jnp.take(jnp.stack(received), order, axis=0)


def tree(items, combine):
    items = list(items)
    while len(items) > 1:
        items = [combine(items[i], items[i + 1]) for i in range(0, len(items), 2)]
    return items[0]


def digits(voc, core):
    z, x = voc % SIDE, voc // SIDE
    return (z, x) if core == 0 else (x, z)


def compose(first, second, core):
    return first * SIDE + second if core else second * SIDE + first


def shift(value, phase, step, reqs, vocs):
    pairs = []
    for req in range(reqs):
        core = req % 2
        for voc in range(vocs):
            ring = list(digits(voc, core))
            ring[phase] = (ring[phase] + step) % SIDE
            pairs.append((req * vocs + voc, req * vocs + compose(ring[0], ring[1], core)))
    return lax.ppermute(value, AXES, pairs)


def block_stats(block, head, position):
    width = head.shape[0]
    shard_width = head.shape[1]
    rows_in = block[:, :width]
    meta = block[:, width:width + 2].astype(jnp.int32)
    ids = meta[:, 0] * 256 + meta[:, 1] - position * shard_width
    columns = jnp.arange(shard_width, dtype=jnp.int32)
    logits = jnp.dot(rows_in, head, preferred_element_type=jnp.float32)
    top = jnp.max(logits, axis=-1)
    expo = jnp.exp(logits - top[:, None])
    total = jnp.sum(expo, axis=-1)
    weighted = jnp.sum(expo * logits, axis=-1)
    picked = jnp.sum(jnp.where(columns[None, :] == ids[:, None], logits, 0.0), axis=-1)
    return jnp.stack([top, total, weighted, picked])


def shards(hidden, norm_gain, head, targets, bounds):
    slots = hidden.shape[0]
    width = hidden.shape[1]
    reqs = lax.axis_size("req")
    vocs = lax.axis_size("voc")
    position = lax.axis_index("voc")
    core = lax.axis_index("req") % 2
    start = bounds[0, 0]
    finish = bounds[0, 1]
    live_count = finish - start
    values = hidden.astype(jnp.float32)
    meansq = jnp.mean(values * values, axis=-1, keepdims=True)
    normed_all = (values * lax.rsqrt(meansq + 1e-05) * norm_gain).astype(jnp.bfloat16)
    normed = lax.dynamic_slice_in_dim(normed_all, start, LIVE, 0)
    ids = lax.dynamic_slice_in_dim(targets, start, LIVE, 0)
    column = lax.broadcasted_iota(jnp.int32, (LIVE, EXTRA), 1)
    meta = jnp.where(column == 0, ids[:, None] // 256, ids[:, None] % 256)
    meta = jnp.where(column == 2, live_count, jnp.where(column < 2, meta, 0))
    own = jnp.concatenate([normed, meta.astype(jnp.bfloat16)], axis=1)

    stats = lambda block: block_stats(block, head, position)
    left = shift(own, 0, 1, reqs, vocs)
    right = shift(own, 0, -1, reqs, vocs)
    part_own = stats(own)
    far = shift(own, 0, 2, reqs, vocs)
    part_near = stats(jnp.concatenate([left, right]))
    line = jnp.stack([own, left, right, far])
    halves = lambda step: jnp.concatenate(
        [shift(line[:, :HALF], 1, step, reqs, vocs), shift(line[:, HALF:], 1, step, reqs, vocs)], axis=1
    )
    line_left = halves(1)
    line_right = halves(-1)
    part_far = stats(far)
    line_far = halves(2)
    part_lines = stats(jnp.concatenate([line_left, line_right]).reshape(-1, own.shape[1]))
    part_line_far = stats(line_far.reshape(-1, own.shape[1]))
    processed = jnp.concatenate([part_own, part_near, part_far, part_lines, part_line_far], axis=1)
    processed = processed.reshape(4, vocs, LIVE)
    count_of = lambda block: block[..., :1, width + 2].reshape(-1).astype(jnp.int32)
    processed_counts = jnp.concatenate(
        [count_of(line), count_of(line_left), count_of(line_right), count_of(line_far)]
    )

    source = jnp.arange(vocs, dtype=jnp.int32)
    slot_of = jnp.array([0, 2, 3, 1], jnp.int32)
    my_a = jnp.where(core == 0, position % SIDE, position // SIDE)
    my_b = jnp.where(core == 0, position // SIDE, position % SIDE)
    src_a = jnp.where(core == 0, source % SIDE, source // SIDE)
    src_b = jnp.where(core == 0, source // SIDE, source % SIDE)
    where_is = slot_of[(src_b - my_b) % SIDE] * SIDE + slot_of[(src_a - my_a) % SIDE]
    canonical = jnp.take(processed, where_is, axis=1).reshape(4, vocs * LIVE)
    counts = jnp.take(processed_counts, where_is, axis=0)

    merged = butterfly(canonical, "voc", combine_stats, (1, 3, 4, 12))
    top, total, weighted, picked = merged[0], merged[1], merged[2], merged[3]
    lse = top + jnp.log(total)
    row_entropy = lse - weighted / total
    row_logprob = picked - lse
    slot = jnp.arange(LIVE, dtype=jnp.int32)
    group_live = slot[None, :] < counts[:, None]
    group_entropy = jnp.where(group_live, row_entropy.reshape(vocs, LIVE), 0.0)
    totals = jnp.stack([jnp.sum(group_entropy), jnp.sum(counts).astype(jnp.float32)])
    totals = butterfly(totals, "req", lambda a, b: a + b, (1, 2, 6))
    mean_entropy = (totals[0] / totals[1]).reshape(1)
    mine = lambda a: lax.dynamic_slice_in_dim(a, position * LIVE, LIVE, 0)
    live = slot < live_count
    zero = jnp.zeros((LIVE,), jnp.float32)
    place = lambda a: lax.dynamic_update_slice_in_dim(jnp.zeros((slots,), jnp.float32), a, start, 0)
    entropy = place(jnp.where(live, mine(row_entropy), zero))
    logprob = place(jnp.where(live, mine(row_logprob), zero))
    target_logit = place(jnp.where(live, mine(picked), zero))
    return (logprob, entropy, target_logit, mean_entropy)


def solution(mesh):
    placed = (
        P(AXES, None),
        P(),
        P(None, "voc"),
        P(AXES),
        P(AXES, None),
    )
    return jax.shard_map(
        shards,
        mesh=mesh,
        in_specs=placed,
        out_specs=(P(AXES), P(AXES), P(AXES), P()),
        check_vma=False,
    )
```

```python
import jax
import jax.numpy as jnp
from jax import lax
from jax.sharding import PartitionSpec as P

LIVE = 96
HALF = LIVE // 2
EXTRA = 128
SIDE = 4
AXES = ("req", "voc")


def combine_stats(first, second):
    top = jnp.maximum(first[0], second[0])
    weight_a = jnp.exp(first[0] - top)
    weight_b = jnp.exp(second[0] - top)
    return jnp.stack(
        [
            top,
            first[1] * weight_a + second[1] * weight_b,
            first[2] * weight_a + second[2] * weight_b,
            first[3] + second[3],
        ]
    )


def butterfly(value, axis, combine, flips):
    size = lax.axis_size(axis)
    index = lax.axis_index(axis)
    step = 1
    for flip in flips:
        other = lax.ppermute(value, axis, [(i, i ^ flip) for i in range(size)])
        upper = (index & step) != 0
        first = jnp.where(upper, other, value)
        second = jnp.where(upper, value, other)
        value = combine(first, second)
        step *= 2
    return value


def members(value, axis, sub, stride):
    size = lax.axis_size(axis)
    digit = (lax.axis_index(axis) // stride) % sub
    received = [value]
    for shift in range(1, sub):
        pairs = []
        for i in range(size):
            d = (i // stride) % sub
            pairs.append((i, i + ((d + shift) % sub - d) * stride))
        received.append(lax.ppermute(value, axis, pairs))
    order = (digit - jnp.arange(sub, dtype=jnp.int32)) % sub
    return jnp.take(jnp.stack(received), order, axis=0)


def tree(items, combine):
    items = list(items)
    while len(items) > 1:
        items = [combine(items[i], items[i + 1]) for i in range(0, len(items), 2)]
    return items[0]


def digits(voc, core):
    z, x = voc % SIDE, voc // SIDE
    return (z, x) if core == 0 else (x, z)


def compose(first, second, core):
    return first * SIDE + second if core else second * SIDE + first


def shift(value, phase, step, reqs, vocs):
    pairs = []
    for req in range(reqs):
        core = req % 2
        for voc in range(vocs):
            ring = list(digits(voc, core))
            ring[phase] = (ring[phase] + step) % SIDE
            pairs.append((req * vocs + voc, req * vocs + compose(ring[0], ring[1], core)))
    return lax.ppermute(value, AXES, pairs)


def block_stats(block, head, position):
    width = head.shape[0]
    shard_width = head.shape[1]
    rows_in = block[:, :width]
    meta = block[:, width:width + 2].astype(jnp.int32)
    ids = meta[:, 0] * 256 + meta[:, 1] - position * shard_width
    columns = jnp.arange(shard_width, dtype=jnp.int32)
    logits = jnp.dot(rows_in, head, preferred_element_type=jnp.float32)
    top = jnp.max(logits, axis=-1)
    expo = jnp.exp(logits - top[:, None])
    total = jnp.sum(expo, axis=-1)
    weighted = jnp.sum(expo * logits, axis=-1)
    picked = jnp.sum(jnp.where(columns[None, :] == ids[:, None], logits, 0.0), axis=-1)
    return jnp.stack([top, total, weighted, picked])


def shards(hidden, norm_gain, head, targets, bounds):
    slots = hidden.shape[0]
    width = hidden.shape[1]
    reqs = lax.axis_size("req")
    vocs = lax.axis_size("voc")
    position = lax.axis_index("voc")
    core = lax.axis_index("req") % 2
    start = bounds[0, 0]
    finish = bounds[0, 1]
    live_count = finish - start
    values = hidden.astype(jnp.float32)
    meansq = jnp.mean(values * values, axis=-1, keepdims=True)
    normed_all = (values * lax.rsqrt(meansq + 1e-05) * norm_gain).astype(jnp.bfloat16)
    pick = (
        lax.broadcasted_iota(jnp.int32, (LIVE, slots), 1)
        == lax.broadcasted_iota(jnp.int32, (LIVE, slots), 0) + start
    )
    normed = jnp.dot(pick.astype(jnp.bfloat16), normed_all, preferred_element_type=jnp.float32)
    normed = normed.astype(jnp.bfloat16)
    ids = jnp.dot(
        pick.astype(jnp.float32), targets.astype(jnp.float32), precision=lax.Precision.HIGHEST
    ).astype(jnp.int32)
    column = lax.broadcasted_iota(jnp.int32, (LIVE, EXTRA), 1)
    meta = jnp.where(column == 0, ids[:, None] // 256, ids[:, None] % 256)
    meta = jnp.where(column == 2, live_count, jnp.where(column < 2, meta, 0))
    own = jnp.concatenate([normed, meta.astype(jnp.bfloat16)], axis=1)

    stats = lambda block: block_stats(block, head, position)
    left = shift(own, 0, 1, reqs, vocs)
    right = shift(own, 0, -1, reqs, vocs)
    part_own = stats(own)
    far = shift(own, 0, 2, reqs, vocs)
    part_near = stats(jnp.concatenate([left, right]))
    line = jnp.stack([own, left, right, far])
    halves = lambda step: jnp.concatenate(
        [shift(line[:, :HALF], 1, step, reqs, vocs), shift(line[:, HALF:], 1, step, reqs, vocs)], axis=1
    )
    line_left = halves(1)
    line_right = halves(-1)
    part_far = stats(far)
    line_far = halves(2)
    part_lines = stats(jnp.concatenate([line_left, line_right]).reshape(-1, own.shape[1]))
    part_line_far = stats(line_far.reshape(-1, own.shape[1]))
    processed = jnp.concatenate([part_own, part_near, part_far, part_lines, part_line_far], axis=1)
    processed = processed.reshape(4, vocs, LIVE)
    count_of = lambda block: block[..., :1, width + 2].reshape(-1).astype(jnp.int32)
    processed_counts = jnp.concatenate(
        [count_of(line), count_of(line_left), count_of(line_right), count_of(line_far)]
    )

    source = jnp.arange(vocs, dtype=jnp.int32)
    slot_of = jnp.array([0, 2, 3, 1], jnp.int32)
    my_a = jnp.where(core == 0, position % SIDE, position // SIDE)
    my_b = jnp.where(core == 0, position // SIDE, position % SIDE)
    src_a = jnp.where(core == 0, source % SIDE, source // SIDE)
    src_b = jnp.where(core == 0, source // SIDE, source % SIDE)
    where_is = slot_of[(src_b - my_b) % SIDE] * SIDE + slot_of[(src_a - my_a) % SIDE]
    canonical = jnp.take(processed, where_is, axis=1).reshape(4, vocs * LIVE)
    counts = jnp.take(processed_counts, where_is, axis=0)

    merged = butterfly(canonical, "voc", combine_stats, (1, 3, 4, 12))
    top, total, weighted, picked = merged[0], merged[1], merged[2], merged[3]
    lse = top + jnp.log(total)
    row_entropy = lse - weighted / total
    row_logprob = picked - lse
    slot = jnp.arange(LIVE, dtype=jnp.int32)
    group_live = slot[None, :] < counts[:, None]
    group_entropy = jnp.where(group_live, row_entropy.reshape(vocs, LIVE), 0.0)
    totals = jnp.stack([jnp.sum(group_entropy), jnp.sum(counts).astype(jnp.float32)])
    totals = butterfly(totals, "req", lambda a, b: a + b, (1, 2, 6))
    mean_entropy = (totals[0] / totals[1]).reshape(1)
    mine = lambda a: lax.dynamic_slice_in_dim(a, position * LIVE, LIVE, 0)
    live = slot < live_count
    zero = jnp.zeros((LIVE,), jnp.float32)
    place = lambda a: lax.dynamic_update_slice_in_dim(jnp.zeros((slots,), jnp.float32), a, start, 0)
    entropy = place(jnp.where(live, mine(row_entropy), zero))
    logprob = place(jnp.where(live, mine(row_logprob), zero))
    target_logit = place(jnp.where(live, mine(picked), zero))
    return (logprob, entropy, target_logit, mean_entropy)


def solution(mesh):
    placed = (
        P(AXES, None),
        P(),
        P(None, "voc"),
        P(AXES),
        P(AXES, None),
    )
    return jax.shard_map(
        shards,
        mesh=mesh,
        in_specs=placed,
        out_specs=(P(AXES), P(AXES), P(AXES), P()),
        check_vma=False,
    )
```

```python
import jax
import jax.numpy as jnp
from jax import lax
from jax.sharding import PartitionSpec as P

LIVE = 96
HALF = LIVE // 2
EXTRA = 128
SIDE = 4
AXES = ("req", "voc")


def combine_stats(first, second):
    top = jnp.maximum(first[0], second[0])
    weight_a = jnp.exp(first[0] - top)
    weight_b = jnp.exp(second[0] - top)
    return jnp.stack(
        [
            top,
            first[1] * weight_a + second[1] * weight_b,
            first[2] * weight_a + second[2] * weight_b,
            first[3] + second[3],
        ]
    )


def butterfly(value, axis, combine, flips):
    size = lax.axis_size(axis)
    index = lax.axis_index(axis)
    step = 1
    for flip in flips:
        other = lax.ppermute(value, axis, [(i, i ^ flip) for i in range(size)])
        upper = (index & step) != 0
        first = jnp.where(upper, other, value)
        second = jnp.where(upper, value, other)
        value = combine(first, second)
        step *= 2
    return value


def members(value, axis, sub, stride):
    size = lax.axis_size(axis)
    digit = (lax.axis_index(axis) // stride) % sub
    received = [value]
    for shift in range(1, sub):
        pairs = []
        for i in range(size):
            d = (i // stride) % sub
            pairs.append((i, i + ((d + shift) % sub - d) * stride))
        received.append(lax.ppermute(value, axis, pairs))
    order = (digit - jnp.arange(sub, dtype=jnp.int32)) % sub
    return jnp.take(jnp.stack(received), order, axis=0)


def tree(items, combine):
    items = list(items)
    while len(items) > 1:
        items = [combine(items[i], items[i + 1]) for i in range(0, len(items), 2)]
    return items[0]


def digits(voc, core):
    z, x = voc % SIDE, voc // SIDE
    return (z, x) if core == 0 else (x, z)


def compose(first, second, core):
    return first * SIDE + second if core else second * SIDE + first


def shift(value, phase, step, reqs, vocs):
    pairs = []
    for req in range(reqs):
        core = req % 2
        for voc in range(vocs):
            ring = list(digits(voc, core))
            ring[phase] = (ring[phase] + step) % SIDE
            pairs.append((req * vocs + voc, req * vocs + compose(ring[0], ring[1], core)))
    return lax.ppermute(value, AXES, pairs)


def block_stats(block, head, position):
    width = head.shape[0]
    shard_width = head.shape[1]
    rows_in = block[:, :width]
    meta = block[:, width:width + 2].astype(jnp.int32)
    ids = meta[:, 0] * 256 + meta[:, 1] - position * shard_width
    columns = jnp.arange(shard_width, dtype=jnp.int32)
    logits = jnp.dot(rows_in, head, preferred_element_type=jnp.float32)
    top = jnp.max(logits, axis=-1)
    expo = jnp.exp(logits - top[:, None])
    total = jnp.sum(expo, axis=-1)
    weighted = jnp.sum(expo * logits, axis=-1)
    picked = jnp.sum(jnp.where(columns[None, :] == ids[:, None], logits, 0.0), axis=-1)
    return jnp.stack([top, total, weighted, picked])


def shards(hidden, norm_gain, head, targets, bounds):
    slots = hidden.shape[0]
    width = hidden.shape[1]
    reqs = lax.axis_size("req")
    vocs = lax.axis_size("voc")
    position = lax.axis_index("voc")
    core = lax.axis_index("req") % 2
    start = bounds[0, 0]
    finish = bounds[0, 1]
    live_count = finish - start
    values = hidden.astype(jnp.float32)
    meansq = jnp.mean(values * values, axis=-1, keepdims=True)
    normed_all = (values * lax.rsqrt(meansq + 1e-05) * norm_gain).astype(jnp.bfloat16)
    pick = (
        lax.broadcasted_iota(jnp.int32, (LIVE, slots), 1)
        == lax.broadcasted_iota(jnp.int32, (LIVE, slots), 0) + start
    )
    normed = jnp.dot(pick.astype(jnp.bfloat16), normed_all, preferred_element_type=jnp.float32)
    normed = normed.astype(jnp.bfloat16)
    ids = jnp.dot(
        pick.astype(jnp.float32), targets.astype(jnp.float32), precision=lax.Precision.HIGHEST
    ).astype(jnp.int32)
    column = lax.broadcasted_iota(jnp.int32, (LIVE, EXTRA), 1)
    meta = jnp.where(column == 0, ids[:, None] // 256, ids[:, None] % 256)
    meta = jnp.where(column == 2, live_count, jnp.where(column < 2, meta, 0))
    own = jnp.concatenate([normed, meta.astype(jnp.bfloat16)], axis=1)

    stats = lambda block: block_stats(block, head, position)
    split = lambda step: jnp.concatenate(
        [shift(own[:HALF], 0, step, reqs, vocs), shift(own[HALF:], 0, step, reqs, vocs)]
    )
    left = split(1)
    right = split(-1)
    part_own = stats(own)
    far = split(2)
    part_near = stats(jnp.concatenate([left, right]))
    line = jnp.stack([own, left, right, far])
    halves = lambda step: jnp.concatenate(
        [shift(line[:, :HALF], 1, step, reqs, vocs), shift(line[:, HALF:], 1, step, reqs, vocs)], axis=1
    )
    line_left = halves(1)
    line_right = halves(-1)
    part_far = stats(far)
    line_far = halves(2)
    part_lines = stats(jnp.concatenate([line_left, line_right]).reshape(-1, own.shape[1]))
    part_line_far = stats(line_far.reshape(-1, own.shape[1]))
    processed = jnp.concatenate([part_own, part_near, part_far, part_lines, part_line_far], axis=1)
    processed = processed.reshape(4, vocs, LIVE)
    count_of = lambda block: block[..., :1, width + 2].reshape(-1).astype(jnp.int32)
    processed_counts = jnp.concatenate(
        [count_of(line), count_of(line_left), count_of(line_right), count_of(line_far)]
    )

    source = jnp.arange(vocs, dtype=jnp.int32)
    slot_of = jnp.array([0, 2, 3, 1], jnp.int32)
    my_a = jnp.where(core == 0, position % SIDE, position // SIDE)
    my_b = jnp.where(core == 0, position // SIDE, position % SIDE)
    src_a = jnp.where(core == 0, source % SIDE, source // SIDE)
    src_b = jnp.where(core == 0, source // SIDE, source % SIDE)
    where_is = slot_of[(src_b - my_b) % SIDE] * SIDE + slot_of[(src_a - my_a) % SIDE]
    canonical = jnp.take(processed, where_is, axis=1).reshape(4, vocs * LIVE)
    counts = jnp.take(processed_counts, where_is, axis=0)

    merged = butterfly(canonical, "voc", combine_stats, (1, 3, 4, 12))
    top, total, weighted, picked = merged[0], merged[1], merged[2], merged[3]
    lse = top + jnp.log(total)
    row_entropy = lse - weighted / total
    row_logprob = picked - lse
    slot = jnp.arange(LIVE, dtype=jnp.int32)
    group_live = slot[None, :] < counts[:, None]
    group_entropy = jnp.where(group_live, row_entropy.reshape(vocs, LIVE), 0.0)
    totals = jnp.stack([jnp.sum(group_entropy), jnp.sum(counts).astype(jnp.float32)])
    totals = butterfly(totals, "req", lambda a, b: a + b, (1, 2, 6))
    mean_entropy = (totals[0] / totals[1]).reshape(1)
    mine = lambda a: lax.dynamic_slice_in_dim(a, position * LIVE, LIVE, 0)
    live = slot < live_count
    zero = jnp.zeros((LIVE,), jnp.float32)
    place = lambda a: lax.dynamic_update_slice_in_dim(jnp.zeros((slots,), jnp.float32), a, start, 0)
    entropy = place(jnp.where(live, mine(row_entropy), zero))
    logprob = place(jnp.where(live, mine(row_logprob), zero))
    target_logit = place(jnp.where(live, mine(picked), zero))
    return (logprob, entropy, target_logit, mean_entropy)


def solution(mesh):
    placed = (
        P(AXES, None),
        P(),
        P(None, "voc"),
        P(AXES),
        P(AXES, None),
    )
    return jax.shard_map(
        shards,
        mesh=mesh,
        in_specs=placed,
        out_specs=(P(AXES), P(AXES), P(AXES), P()),
        check_vma=False,
    )
```

```python
import jax
import jax.numpy as jnp
from jax import lax
from jax.sharding import PartitionSpec as P

LIVE = 96
HALF = LIVE // 2
EXTRA = 128
SIDE = 4
AXES = ("req", "voc")


def combine_stats(first, second):
    top = jnp.maximum(first[0], second[0])
    weight_a = jnp.exp(first[0] - top)
    weight_b = jnp.exp(second[0] - top)
    return jnp.stack(
        [
            top,
            first[1] * weight_a + second[1] * weight_b,
            first[2] * weight_a + second[2] * weight_b,
            first[3] + second[3],
        ]
    )


def butterfly(value, axis, combine, flips):
    size = lax.axis_size(axis)
    index = lax.axis_index(axis)
    step = 1
    for flip in flips:
        other = lax.ppermute(value, axis, [(i, i ^ flip) for i in range(size)])
        upper = (index & step) != 0
        first = jnp.where(upper, other, value)
        second = jnp.where(upper, value, other)
        value = combine(first, second)
        step *= 2
    return value


def members(value, axis, sub, stride):
    size = lax.axis_size(axis)
    digit = (lax.axis_index(axis) // stride) % sub
    received = [value]
    for shift in range(1, sub):
        pairs = []
        for i in range(size):
            d = (i // stride) % sub
            pairs.append((i, i + ((d + shift) % sub - d) * stride))
        received.append(lax.ppermute(value, axis, pairs))
    order = (digit - jnp.arange(sub, dtype=jnp.int32)) % sub
    return jnp.take(jnp.stack(received), order, axis=0)


def tree(items, combine):
    items = list(items)
    while len(items) > 1:
        items = [combine(items[i], items[i + 1]) for i in range(0, len(items), 2)]
    return items[0]


def digits(voc, core):
    z, x = voc % SIDE, voc // SIDE
    return (z, x) if core == 0 else (x, z)


def compose(first, second, core):
    return first * SIDE + second if core else second * SIDE + first


def shift(value, phase, step, reqs, vocs):
    pairs = []
    for req in range(reqs):
        core = req % 2
        for voc in range(vocs):
            ring = list(digits(voc, core))
            ring[phase] = (ring[phase] + step) % SIDE
            pairs.append((req * vocs + voc, req * vocs + compose(ring[0], ring[1], core)))
    return lax.ppermute(value, AXES, pairs)


def block_stats(block, head, position):
    width = head.shape[0]
    shard_width = head.shape[1]
    rows_in = block[:, :width]
    meta = block[:, width:width + 2].astype(jnp.int32)
    ids = meta[:, 0] * 256 + meta[:, 1] - position * shard_width
    columns = jnp.arange(shard_width, dtype=jnp.int32)
    logits = jnp.dot(rows_in, head, preferred_element_type=jnp.float32)
    top = jnp.max(logits, axis=-1)
    expo = jnp.exp(logits - top[:, None])
    total = jnp.sum(expo, axis=-1)
    weighted = jnp.sum(expo * logits, axis=-1)
    picked = jnp.sum(jnp.where(columns[None, :] == ids[:, None], logits, 0.0), axis=-1)
    return jnp.stack([top, total, weighted, picked])


def shards(hidden, norm_gain, head, targets, bounds):
    slots = hidden.shape[0]
    width = hidden.shape[1]
    reqs = lax.axis_size("req")
    vocs = lax.axis_size("voc")
    position = lax.axis_index("voc")
    core = lax.axis_index("req") % 2
    start = bounds[0, 0]
    finish = bounds[0, 1]
    live_count = finish - start
    values = hidden.astype(jnp.float32)
    meansq = jnp.mean(values * values, axis=-1, keepdims=True)
    normed_all = (values * lax.rsqrt(meansq + 1e-05) * norm_gain).astype(jnp.bfloat16)
    pick = (
        lax.broadcasted_iota(jnp.int32, (LIVE, slots), 1)
        == lax.broadcasted_iota(jnp.int32, (LIVE, slots), 0) + start
    )
    normed = jnp.dot(pick.astype(jnp.bfloat16), normed_all, preferred_element_type=jnp.float32)
    normed = normed.astype(jnp.bfloat16)
    ids = jnp.dot(
        pick.astype(jnp.float32), targets.astype(jnp.float32), precision=lax.Precision.HIGHEST
    ).astype(jnp.int32)
    column = lax.broadcasted_iota(jnp.int32, (LIVE, EXTRA), 1)
    meta = jnp.where(column == 0, ids[:, None] // 256, ids[:, None] % 256)
    meta = jnp.where(column == 2, live_count, jnp.where(column < 2, meta, 0))
    own = jnp.concatenate([normed, meta.astype(jnp.bfloat16)], axis=1)

    stats = lambda block: block_stats(block, head, position)
    left = shift(own, 0, 1, reqs, vocs)
    right = shift(own, 0, -1, reqs, vocs)
    part_own = stats(own)
    far = shift(own, 0, 2, reqs, vocs)
    part_near = stats(jnp.concatenate([left, right]))
    line = jnp.stack([own, left, right, far])
    halves = lambda step: jnp.concatenate(
        [shift(line[:, :HALF], 1, step, reqs, vocs), shift(line[:, HALF:], 1, step, reqs, vocs)], axis=1
    )
    line_left = halves(1)
    line_right = halves(-1)
    part_far = stats(far)
    part_near, part_far, line = lax.optimization_barrier((part_near, part_far, line))
    line_far = halves(2)
    part_lines = stats(jnp.concatenate([line_left, line_right]).reshape(-1, own.shape[1]))
    part_lines, line_far = lax.optimization_barrier((part_lines, line_far))
    part_line_far = stats(line_far.reshape(-1, own.shape[1]))
    processed = jnp.concatenate([part_own, part_near, part_far, part_lines, part_line_far], axis=1)
    processed = processed.reshape(4, vocs, LIVE)
    count_of = lambda block: block[..., :1, width + 2].reshape(-1).astype(jnp.int32)
    processed_counts = jnp.concatenate(
        [count_of(line), count_of(line_left), count_of(line_right), count_of(line_far)]
    )

    source = jnp.arange(vocs, dtype=jnp.int32)
    slot_of = jnp.array([0, 2, 3, 1], jnp.int32)
    my_a = jnp.where(core == 0, position % SIDE, position // SIDE)
    my_b = jnp.where(core == 0, position // SIDE, position % SIDE)
    src_a = jnp.where(core == 0, source % SIDE, source // SIDE)
    src_b = jnp.where(core == 0, source // SIDE, source % SIDE)
    where_is = slot_of[(src_b - my_b) % SIDE] * SIDE + slot_of[(src_a - my_a) % SIDE]
    canonical = jnp.take(processed, where_is, axis=1).reshape(4, vocs * LIVE)
    counts = jnp.take(processed_counts, where_is, axis=0)

    merged = butterfly(canonical, "voc", combine_stats, (1, 3, 4, 12))
    top, total, weighted, picked = merged[0], merged[1], merged[2], merged[3]
    lse = top + jnp.log(total)
    row_entropy = lse - weighted / total
    row_logprob = picked - lse
    slot = jnp.arange(LIVE, dtype=jnp.int32)
    group_live = slot[None, :] < counts[:, None]
    group_entropy = jnp.where(group_live, row_entropy.reshape(vocs, LIVE), 0.0)
    totals = jnp.stack([jnp.sum(group_entropy), jnp.sum(counts).astype(jnp.float32)])
    totals = butterfly(totals, "req", lambda a, b: a + b, (1, 2, 6))
    mean_entropy = (totals[0] / totals[1]).reshape(1)
    mine = lambda a: lax.dynamic_slice_in_dim(a, position * LIVE, LIVE, 0)
    live = slot < live_count
    zero = jnp.zeros((LIVE,), jnp.float32)
    place = lambda a: lax.dynamic_update_slice_in_dim(jnp.zeros((slots,), jnp.float32), a, start, 0)
    entropy = place(jnp.where(live, mine(row_entropy), zero))
    logprob = place(jnp.where(live, mine(row_logprob), zero))
    target_logit = place(jnp.where(live, mine(picked), zero))
    return (logprob, entropy, target_logit, mean_entropy)


def solution(mesh):
    placed = (
        P(AXES, None),
        P(),
        P(None, "voc"),
        P(AXES),
        P(AXES, None),
    )
    return jax.shard_map(
        shards,
        mesh=mesh,
        in_specs=placed,
        out_specs=(P(AXES), P(AXES), P(AXES), P()),
        check_vma=False,
    )
```

```python
import jax
import jax.numpy as jnp
from jax import lax
from jax.sharding import PartitionSpec as P

LIVE = 96
HALF = LIVE // 2
EXTRA = 128
SIDE = 4
AXES = ("req", "voc")


def combine_stats(first, second):
    top = jnp.maximum(first[0], second[0])
    weight_a = jnp.exp(first[0] - top)
    weight_b = jnp.exp(second[0] - top)
    return jnp.stack(
        [
            top,
            first[1] * weight_a + second[1] * weight_b,
            first[2] * weight_a + second[2] * weight_b,
            first[3] + second[3],
        ]
    )


def butterfly(value, axis, combine, flips):
    size = lax.axis_size(axis)
    index = lax.axis_index(axis)
    step = 1
    for flip in flips:
        other = lax.ppermute(value, axis, [(i, i ^ flip) for i in range(size)])
        upper = (index & step) != 0
        first = jnp.where(upper, other, value)
        second = jnp.where(upper, value, other)
        value = combine(first, second)
        step *= 2
    return value


def members(value, axis, sub, stride):
    size = lax.axis_size(axis)
    digit = (lax.axis_index(axis) // stride) % sub
    received = [value]
    for shift in range(1, sub):
        pairs = []
        for i in range(size):
            d = (i // stride) % sub
            pairs.append((i, i + ((d + shift) % sub - d) * stride))
        received.append(lax.ppermute(value, axis, pairs))
    order = (digit - jnp.arange(sub, dtype=jnp.int32)) % sub
    return jnp.take(jnp.stack(received), order, axis=0)


def tree(items, combine):
    items = list(items)
    while len(items) > 1:
        items = [combine(items[i], items[i + 1]) for i in range(0, len(items), 2)]
    return items[0]


def digits(voc, core):
    z, x = voc % SIDE, voc // SIDE
    return (z, x) if core == 0 else (x, z)


def compose(first, second, core):
    return first * SIDE + second if core else second * SIDE + first


def shift(value, phase, step, reqs, vocs):
    pairs = []
    for req in range(reqs):
        core = req % 2
        for voc in range(vocs):
            ring = list(digits(voc, core))
            ring[phase] = (ring[phase] + step) % SIDE
            pairs.append((req * vocs + voc, req * vocs + compose(ring[0], ring[1], core)))
    return lax.ppermute(value, AXES, pairs)


def block_stats(block, head, position):
    width = head.shape[0]
    shard_width = head.shape[1]
    rows_in = block[:, :width]
    meta = block[:, width:width + 2].astype(jnp.int32)
    ids = meta[:, 0] * 256 + meta[:, 1] - position * shard_width
    columns = jnp.arange(shard_width, dtype=jnp.int32)
    logits = jnp.dot(rows_in, head, preferred_element_type=jnp.float32)
    top = jnp.max(logits, axis=-1)
    expo = jnp.exp(logits - top[:, None])
    total = jnp.sum(expo, axis=-1)
    weighted = jnp.sum(expo * logits, axis=-1)
    picked = jnp.sum(jnp.where(columns[None, :] == ids[:, None], logits, 0.0), axis=-1)
    return jnp.stack([top, total, weighted, picked])


def shards(hidden, norm_gain, head, targets, bounds):
    slots = hidden.shape[0]
    width = hidden.shape[1]
    reqs = lax.axis_size("req")
    vocs = lax.axis_size("voc")
    position = lax.axis_index("voc")
    core = lax.axis_index("req") % 2
    start = bounds[0, 0]
    finish = bounds[0, 1]
    live_count = finish - start
    values = hidden.astype(jnp.float32)
    meansq = jnp.mean(values * values, axis=-1, keepdims=True)
    normed_all = (values * lax.rsqrt(meansq + 1e-05) * norm_gain).astype(jnp.bfloat16)
    pick = (
        lax.broadcasted_iota(jnp.int32, (LIVE, slots), 1)
        == lax.broadcasted_iota(jnp.int32, (LIVE, slots), 0) + start
    )
    normed = jnp.dot(pick.astype(jnp.bfloat16), normed_all, preferred_element_type=jnp.float32)
    normed = normed.astype(jnp.bfloat16)
    ids = jnp.dot(
        pick.astype(jnp.float32), targets.astype(jnp.float32), precision=lax.Precision.HIGHEST
    ).astype(jnp.int32)
    column = lax.broadcasted_iota(jnp.int32, (LIVE, EXTRA), 1)
    meta = jnp.where(column == 0, ids[:, None] // 256, ids[:, None] % 256)
    meta = jnp.where(column == 2, live_count, jnp.where(column < 2, meta, 0))
    own = jnp.concatenate([normed, meta.astype(jnp.bfloat16)], axis=1)

    stats = lambda block: block_stats(block, head, position)
    left = shift(own, 0, 1, reqs, vocs)
    right = shift(own, 0, -1, reqs, vocs)
    part_own = stats(own)
    far = shift(own, 0, 2, reqs, vocs)
    part_near = stats(jnp.concatenate([left, right]))
    line = jnp.stack([own, left, right, far])
    halves = lambda step: jnp.concatenate(
        [shift(line[:, :HALF], 1, step, reqs, vocs), shift(line[:, HALF:], 1, step, reqs, vocs)], axis=1
    )
    line_left = halves(1)
    line_right = halves(-1)
    part_far = stats(far)
    line_far = halves(2)
    part_lines = stats(jnp.concatenate([line_left, line_right]).reshape(-1, own.shape[1]))
    part_line_far = stats(line_far.reshape(-1, own.shape[1]))
    processed = jnp.concatenate([part_own, part_near, part_far, part_lines, part_line_far], axis=1)
    processed = processed.reshape(4, vocs, LIVE)
    count_of = lambda block: block[..., :1, width + 2].reshape(-1).astype(jnp.int32)
    processed_counts = jnp.concatenate(
        [count_of(line), count_of(line_left), count_of(line_right), count_of(line_far)]
    )

    source = jnp.arange(vocs, dtype=jnp.int32)
    slot_of = jnp.array([0, 2, 3, 1], jnp.int32)
    my_a = jnp.where(core == 0, position % SIDE, position // SIDE)
    my_b = jnp.where(core == 0, position // SIDE, position % SIDE)
    src_a = jnp.where(core == 0, source % SIDE, source // SIDE)
    src_b = jnp.where(core == 0, source // SIDE, source % SIDE)
    where_is = slot_of[(src_b - my_b) % SIDE] * SIDE + slot_of[(src_a - my_a) % SIDE]
    canonical = jnp.take(processed, where_is, axis=1).reshape(4, vocs * LIVE)
    counts = jnp.take(processed_counts, where_is, axis=0)

    merged = butterfly(canonical, "voc", combine_stats, (1, 3, 4, 12))
    top, total, weighted, picked = merged[0], merged[1], merged[2], merged[3]
    lse = top + jnp.log(total)
    row_entropy = lse - weighted / total
    row_logprob = picked - lse
    slot = jnp.arange(LIVE, dtype=jnp.int32)
    group_live = slot[None, :] < counts[:, None]
    group_entropy = jnp.where(group_live, row_entropy.reshape(vocs, LIVE), 0.0)
    totals = jnp.stack([jnp.sum(group_entropy), jnp.sum(counts).astype(jnp.float32)])
    totals = lax.psum(totals, "req")
    mean_entropy = (totals[0] / totals[1]).reshape(1)
    mine = lambda a: lax.dynamic_slice_in_dim(a, position * LIVE, LIVE, 0)
    live = slot < live_count
    zero = jnp.zeros((LIVE,), jnp.float32)
    place = lambda a: lax.dynamic_update_slice_in_dim(jnp.zeros((slots,), jnp.float32), a, start, 0)
    entropy = place(jnp.where(live, mine(row_entropy), zero))
    logprob = place(jnp.where(live, mine(row_logprob), zero))
    target_logit = place(jnp.where(live, mine(picked), zero))
    return (logprob, entropy, target_logit, mean_entropy)


def solution(mesh):
    placed = (
        P(AXES, None),
        P(),
        P(None, "voc"),
        P(AXES),
        P(AXES, None),
    )
    return jax.shard_map(
        shards,
        mesh=mesh,
        in_specs=placed,
        out_specs=(P(AXES), P(AXES), P(AXES), P()),
        check_vma=False,
    )
```

```python
import jax
import jax.numpy as jnp
from jax import lax
from jax.sharding import PartitionSpec as P

LIVE = 96
HALF = LIVE // 2
EXTRA = 128
SIDE = 4
AXES = ("req", "voc")


def combine_stats(first, second):
    top = jnp.maximum(first[0], second[0])
    weight_a = jnp.exp(first[0] - top)
    weight_b = jnp.exp(second[0] - top)
    return jnp.stack(
        [
            top,
            first[1] * weight_a + second[1] * weight_b,
            first[2] * weight_a + second[2] * weight_b,
            first[3] + second[3],
        ]
    )


def butterfly(value, axis, combine, flips):
    size = lax.axis_size(axis)
    index = lax.axis_index(axis)
    step = 1
    for flip in flips:
        other = lax.ppermute(value, axis, [(i, i ^ flip) for i in range(size)])
        upper = (index & step) != 0
        first = jnp.where(upper, other, value)
        second = jnp.where(upper, value, other)
        value = combine(first, second)
        step *= 2
    return value


def members(value, axis, sub, stride):
    size = lax.axis_size(axis)
    digit = (lax.axis_index(axis) // stride) % sub
    received = [value]
    for shift in range(1, sub):
        pairs = []
        for i in range(size):
            d = (i // stride) % sub
            pairs.append((i, i + ((d + shift) % sub - d) * stride))
        received.append(lax.ppermute(value, axis, pairs))
    order = (digit - jnp.arange(sub, dtype=jnp.int32)) % sub
    return jnp.take(jnp.stack(received), order, axis=0)


def tree(items, combine):
    items = list(items)
    while len(items) > 1:
        items = [combine(items[i], items[i + 1]) for i in range(0, len(items), 2)]
    return items[0]


def digits(voc, core):
    z, x = voc % SIDE, voc // SIDE
    return (z, x) if core == 0 else (x, z)


def compose(first, second, core):
    return first * SIDE + second if core else second * SIDE + first


def shift(value, phase, step, reqs, vocs):
    pairs = []
    for req in range(reqs):
        core = req % 2
        for voc in range(vocs):
            ring = list(digits(voc, core))
            ring[phase] = (ring[phase] + step) % SIDE
            pairs.append((req * vocs + voc, req * vocs + compose(ring[0], ring[1], core)))
    return lax.ppermute(value, AXES, pairs)


def block_stats(block, head, position):
    width = head.shape[0]
    shard_width = head.shape[1]
    rows_in = block[:, :width]
    meta = block[:, width:width + 2].astype(jnp.int32)
    ids = meta[:, 0] * 256 + meta[:, 1] - position * shard_width
    columns = jnp.arange(shard_width, dtype=jnp.int32)
    logits = jnp.dot(rows_in, head, preferred_element_type=jnp.float32)
    top = jnp.max(logits, axis=-1)
    expo = jnp.exp(logits - top[:, None])
    total = jnp.sum(expo, axis=-1)
    weighted = jnp.sum(expo * logits, axis=-1)
    picked = jnp.sum(jnp.where(columns[None, :] == ids[:, None], logits, 0.0), axis=-1)
    return jnp.stack([top, total, weighted, picked])


def shards(hidden, norm_gain, head, targets, bounds):
    slots = hidden.shape[0]
    width = hidden.shape[1]
    reqs = lax.axis_size("req")
    vocs = lax.axis_size("voc")
    position = lax.axis_index("voc")
    core = lax.axis_index("req") % 2
    start = bounds[0, 0]
    finish = bounds[0, 1]
    live_count = finish - start
    values = hidden.astype(jnp.float32)
    meansq = jnp.mean(values * values, axis=-1, keepdims=True)
    normed_all = (values * lax.rsqrt(meansq + 1e-05) * norm_gain).astype(jnp.bfloat16)
    pick = (
        lax.broadcasted_iota(jnp.int32, (LIVE, slots), 1)
        == lax.broadcasted_iota(jnp.int32, (LIVE, slots), 0) + start
    )
    normed = jnp.dot(pick.astype(jnp.bfloat16), normed_all, preferred_element_type=jnp.float32)
    normed = normed.astype(jnp.bfloat16)
    ids = jnp.dot(
        pick.astype(jnp.float32), targets.astype(jnp.float32), precision=lax.Precision.HIGHEST
    ).astype(jnp.int32)
    column = lax.broadcasted_iota(jnp.int32, (LIVE, EXTRA), 1)
    meta = jnp.where(column == 0, ids[:, None] // 256, ids[:, None] % 256)
    meta = jnp.where(column == 2, live_count, jnp.where(column < 2, meta, 0))
    own = jnp.concatenate([normed, meta.astype(jnp.bfloat16)], axis=1)

    stats = lambda block: block_stats(block, head, position)
    left = shift(own, 0, 1, reqs, vocs)
    right = shift(own, 0, -1, reqs, vocs)
    far = shift(own, 0, 2, reqs, vocs)
    part_near = stats(jnp.concatenate([own, left, right]))
    line = jnp.stack([own, left, right, far])
    halves = lambda step: jnp.concatenate(
        [shift(line[:, :HALF], 1, step, reqs, vocs), shift(line[:, HALF:], 1, step, reqs, vocs)], axis=1
    )
    line_left = halves(1)
    line_right = halves(-1)
    part_far = stats(far)
    line_far = halves(2)
    part_lines = stats(jnp.concatenate([line_left, line_right]).reshape(-1, own.shape[1]))
    part_line_far = stats(line_far.reshape(-1, own.shape[1]))
    processed = jnp.concatenate([part_near, part_far, part_lines, part_line_far], axis=1)
    processed = processed.reshape(4, vocs, LIVE)
    count_of = lambda block: block[..., :1, width + 2].reshape(-1).astype(jnp.int32)
    processed_counts = jnp.concatenate(
        [count_of(line), count_of(line_left), count_of(line_right), count_of(line_far)]
    )

    source = jnp.arange(vocs, dtype=jnp.int32)
    slot_of = jnp.array([0, 2, 3, 1], jnp.int32)
    my_a = jnp.where(core == 0, position % SIDE, position // SIDE)
    my_b = jnp.where(core == 0, position // SIDE, position % SIDE)
    src_a = jnp.where(core == 0, source % SIDE, source // SIDE)
    src_b = jnp.where(core == 0, source // SIDE, source % SIDE)
    where_is = slot_of[(src_b - my_b) % SIDE] * SIDE + slot_of[(src_a - my_a) % SIDE]
    canonical = jnp.take(processed, where_is, axis=1).reshape(4, vocs * LIVE)
    counts = jnp.take(processed_counts, where_is, axis=0)

    merged = butterfly(canonical, "voc", combine_stats, (1, 3, 4, 12))
    top, total, weighted, picked = merged[0], merged[1], merged[2], merged[3]
    lse = top + jnp.log(total)
    row_entropy = lse - weighted / total
    row_logprob = picked - lse
    slot = jnp.arange(LIVE, dtype=jnp.int32)
    group_live = slot[None, :] < counts[:, None]
    group_entropy = jnp.where(group_live, row_entropy.reshape(vocs, LIVE), 0.0)
    totals = jnp.stack([jnp.sum(group_entropy), jnp.sum(counts).astype(jnp.float32)])
    totals = butterfly(totals, "req", lambda a, b: a + b, (1, 2, 6))
    mean_entropy = (totals[0] / totals[1]).reshape(1)
    mine = lambda a: lax.dynamic_slice_in_dim(a, position * LIVE, LIVE, 0)
    live = slot < live_count
    zero = jnp.zeros((LIVE,), jnp.float32)
    place = lambda a: lax.dynamic_update_slice_in_dim(jnp.zeros((slots,), jnp.float32), a, start, 0)
    entropy = place(jnp.where(live, mine(row_entropy), zero))
    logprob = place(jnp.where(live, mine(row_logprob), zero))
    target_logit = place(jnp.where(live, mine(picked), zero))
    return (logprob, entropy, target_logit, mean_entropy)


def solution(mesh):
    placed = (
        P(AXES, None),
        P(),
        P(None, "voc"),
        P(AXES),
        P(AXES, None),
    )
    return jax.shard_map(
        shards,
        mesh=mesh,
        in_specs=placed,
        out_specs=(P(AXES), P(AXES), P(AXES), P()),
        check_vma=False,
    )
```

```python
import jax
import jax.numpy as jnp
from jax import lax
from jax.sharding import PartitionSpec as P

LIVE = 96
HALF = LIVE // 2
EXTRA = 128
SIDE = 4
AXES = ("req", "voc")


def combine_stats(first, second):
    top = jnp.maximum(first[0], second[0])
    weight_a = jnp.exp(first[0] - top)
    weight_b = jnp.exp(second[0] - top)
    return jnp.stack(
        [
            top,
            first[1] * weight_a + second[1] * weight_b,
            first[2] * weight_a + second[2] * weight_b,
            first[3] + second[3],
        ]
    )


def butterfly(value, axis, combine, flips):
    size = lax.axis_size(axis)
    index = lax.axis_index(axis)
    step = 1
    for flip in flips:
        other = lax.ppermute(value, axis, [(i, i ^ flip) for i in range(size)])
        upper = (index & step) != 0
        first = jnp.where(upper, other, value)
        second = jnp.where(upper, value, other)
        value = combine(first, second)
        step *= 2
    return value


def members(value, axis, sub, stride):
    size = lax.axis_size(axis)
    digit = (lax.axis_index(axis) // stride) % sub
    received = [value]
    for shift in range(1, sub):
        pairs = []
        for i in range(size):
            d = (i // stride) % sub
            pairs.append((i, i + ((d + shift) % sub - d) * stride))
        received.append(lax.ppermute(value, axis, pairs))
    order = (digit - jnp.arange(sub, dtype=jnp.int32)) % sub
    return jnp.take(jnp.stack(received), order, axis=0)


def tree(items, combine):
    items = list(items)
    while len(items) > 1:
        items = [combine(items[i], items[i + 1]) for i in range(0, len(items), 2)]
    return items[0]


def digits(voc, core):
    z, x = voc % SIDE, voc // SIDE
    return (z, x) if core == 0 else (x, z)


def compose(first, second, core):
    return first * SIDE + second if core else second * SIDE + first


def shift(value, phase, step, reqs, vocs):
    pairs = []
    for req in range(reqs):
        core = req % 2
        for voc in range(vocs):
            ring = list(digits(voc, core))
            ring[phase] = (ring[phase] + step) % SIDE
            pairs.append((req * vocs + voc, req * vocs + compose(ring[0], ring[1], core)))
    return lax.ppermute(value, AXES, pairs)


def block_stats(block, head, position):
    width = head.shape[0]
    shard_width = head.shape[1]
    rows_in = block[:, :width]
    meta = block[:, width:width + 2].astype(jnp.int32)
    ids = meta[:, 0] * 256 + meta[:, 1] - position * shard_width
    columns = jnp.arange(shard_width, dtype=jnp.int32)
    logits = jnp.dot(rows_in, head, preferred_element_type=jnp.float32)
    top = jnp.max(logits, axis=-1)
    expo = jnp.exp(logits - top[:, None])
    total = jnp.sum(expo, axis=-1)
    weighted = jnp.sum(expo * logits, axis=-1)
    picked = jnp.sum(jnp.where(columns[None, :] == ids[:, None], logits, 0.0), axis=-1)
    return jnp.stack([top, total, weighted, picked])


def shards(hidden, norm_gain, head, targets, bounds):
    slots = hidden.shape[0]
    width = hidden.shape[1]
    reqs = lax.axis_size("req")
    vocs = lax.axis_size("voc")
    position = lax.axis_index("voc")
    core = lax.axis_index("req") % 2
    start = bounds[0, 0]
    finish = bounds[0, 1]
    live_count = finish - start
    values = hidden.astype(jnp.float32)
    meansq = jnp.mean(values * values, axis=-1, keepdims=True)
    normed_all = (values * lax.rsqrt(meansq + 1e-05) * norm_gain).astype(jnp.bfloat16)
    pick = (
        lax.broadcasted_iota(jnp.int32, (LIVE, slots), 1)
        == lax.broadcasted_iota(jnp.int32, (LIVE, slots), 0) + start
    )
    normed = jnp.dot(pick.astype(jnp.bfloat16), normed_all, preferred_element_type=jnp.float32)
    normed = normed.astype(jnp.bfloat16)
    ids = jnp.dot(
        pick.astype(jnp.float32), targets.astype(jnp.float32), precision=lax.Precision.HIGHEST
    ).astype(jnp.int32)
    column = lax.broadcasted_iota(jnp.int32, (LIVE, EXTRA), 1)
    meta = jnp.where(column == 0, ids[:, None] // 256, ids[:, None] % 256)
    meta = jnp.where(column == 2, live_count, jnp.where(column < 2, meta, 0))
    own = jnp.concatenate([normed, meta.astype(jnp.bfloat16)], axis=1)

    stats = lambda block: block_stats(block, head, position)
    left = shift(own, 0, 1, reqs, vocs)
    right = shift(own, 0, -1, reqs, vocs)
    far = shift(own, 0, 2, reqs, vocs)
    line = jnp.stack([own, left, right, far])
    halves = lambda step: jnp.concatenate(
        [shift(line[:, :HALF], 1, step, reqs, vocs), shift(line[:, HALF:], 1, step, reqs, vocs)], axis=1
    )
    line_left = halves(1)
    line_right = halves(-1)
    part_near = stats(line.reshape(-1, own.shape[1]))
    line_far = halves(2)
    part_lines = stats(jnp.concatenate([line_left, line_right]).reshape(-1, own.shape[1]))
    part_line_far = stats(line_far.reshape(-1, own.shape[1]))
    processed = jnp.concatenate([part_near, part_lines, part_line_far], axis=1)
    processed = processed.reshape(4, vocs, LIVE)
    count_of = lambda block: block[..., :1, width + 2].reshape(-1).astype(jnp.int32)
    processed_counts = jnp.concatenate(
        [count_of(line), count_of(line_left), count_of(line_right), count_of(line_far)]
    )

    source = jnp.arange(vocs, dtype=jnp.int32)
    slot_of = jnp.array([0, 2, 3, 1], jnp.int32)
    my_a = jnp.where(core == 0, position % SIDE, position // SIDE)
    my_b = jnp.where(core == 0, position // SIDE, position % SIDE)
    src_a = jnp.where(core == 0, source % SIDE, source // SIDE)
    src_b = jnp.where(core == 0, source // SIDE, source % SIDE)
    where_is = slot_of[(src_b - my_b) % SIDE] * SIDE + slot_of[(src_a - my_a) % SIDE]
    canonical = jnp.take(processed, where_is, axis=1).reshape(4, vocs * LIVE)
    counts = jnp.take(processed_counts, where_is, axis=0)

    merged = butterfly(canonical, "voc", combine_stats, (1, 3, 4, 12))
    top, total, weighted, picked = merged[0], merged[1], merged[2], merged[3]
    lse = top + jnp.log(total)
    row_entropy = lse - weighted / total
    row_logprob = picked - lse
    slot = jnp.arange(LIVE, dtype=jnp.int32)
    group_live = slot[None, :] < counts[:, None]
    group_entropy = jnp.where(group_live, row_entropy.reshape(vocs, LIVE), 0.0)
    totals = jnp.stack([jnp.sum(group_entropy), jnp.sum(counts).astype(jnp.float32)])
    totals = butterfly(totals, "req", lambda a, b: a + b, (1, 2, 6))
    mean_entropy = (totals[0] / totals[1]).reshape(1)
    mine = lambda a: lax.dynamic_slice_in_dim(a, position * LIVE, LIVE, 0)
    live = slot < live_count
    zero = jnp.zeros((LIVE,), jnp.float32)
    place = lambda a: lax.dynamic_update_slice_in_dim(jnp.zeros((slots,), jnp.float32), a, start, 0)
    entropy = place(jnp.where(live, mine(row_entropy), zero))
    logprob = place(jnp.where(live, mine(row_logprob), zero))
    target_logit = place(jnp.where(live, mine(picked), zero))
    return (logprob, entropy, target_logit, mean_entropy)


def solution(mesh):
    placed = (
        P(AXES, None),
        P(),
        P(None, "voc"),
        P(AXES),
        P(AXES, None),
    )
    return jax.shard_map(
        shards,
        mesh=mesh,
        in_specs=placed,
        out_specs=(P(AXES), P(AXES), P(AXES), P()),
        check_vma=False,
    )
```

```python
import jax
import jax.numpy as jnp
from jax import lax
from jax.sharding import PartitionSpec as P

LIVE = 96
HALF = LIVE // 2
EXTRA = 128
SIDE = 4
AXES = ("req", "voc")


def combine_stats(first, second):
    top = jnp.maximum(first[0], second[0])
    weight_a = jnp.exp(first[0] - top)
    weight_b = jnp.exp(second[0] - top)
    return jnp.stack(
        [
            top,
            first[1] * weight_a + second[1] * weight_b,
            first[2] * weight_a + second[2] * weight_b,
            first[3] + second[3],
        ]
    )


def butterfly(value, axis, combine, flips):
    size = lax.axis_size(axis)
    index = lax.axis_index(axis)
    step = 1
    for flip in flips:
        other = lax.ppermute(value, axis, [(i, i ^ flip) for i in range(size)])
        upper = (index & step) != 0
        first = jnp.where(upper, other, value)
        second = jnp.where(upper, value, other)
        value = combine(first, second)
        step *= 2
    return value


def members(value, axis, sub, stride):
    size = lax.axis_size(axis)
    digit = (lax.axis_index(axis) // stride) % sub
    received = [value]
    for shift in range(1, sub):
        pairs = []
        for i in range(size):
            d = (i // stride) % sub
            pairs.append((i, i + ((d + shift) % sub - d) * stride))
        received.append(lax.ppermute(value, axis, pairs))
    order = (digit - jnp.arange(sub, dtype=jnp.int32)) % sub
    return jnp.take(jnp.stack(received), order, axis=0)


def tree(items, combine):
    items = list(items)
    while len(items) > 1:
        items = [combine(items[i], items[i + 1]) for i in range(0, len(items), 2)]
    return items[0]


def digits(voc, core):
    z, x = voc % SIDE, voc // SIDE
    return (z, x) if core == 0 else (x, z)


def compose(first, second, core):
    return first * SIDE + second if core else second * SIDE + first


def shift(value, phase, step, reqs, vocs):
    pairs = []
    for req in range(reqs):
        core = req % 2
        for voc in range(vocs):
            ring = list(digits(voc, core))
            ring[phase] = (ring[phase] + step) % SIDE
            pairs.append((req * vocs + voc, req * vocs + compose(ring[0], ring[1], core)))
    return lax.ppermute(value, AXES, pairs)


def block_stats(block, head, position):
    width = head.shape[0]
    shard_width = head.shape[1]
    rows_in = block[:, :width]
    meta = block[:, width:width + 2].astype(jnp.int32)
    ids = meta[:, 0] * 256 + meta[:, 1] - position * shard_width
    columns = jnp.arange(shard_width, dtype=jnp.int32)
    logits = jnp.dot(rows_in, head, preferred_element_type=jnp.float32)
    top = jnp.max(logits, axis=-1)
    expo = jnp.exp(logits - top[:, None])
    total = jnp.sum(expo, axis=-1)
    weighted = jnp.sum(expo * logits, axis=-1)
    picked = jnp.sum(jnp.where(columns[None, :] == ids[:, None], logits, 0.0), axis=-1)
    return jnp.stack([top, total, weighted, picked])


def shards(hidden, norm_gain, head, targets, bounds):
    slots = hidden.shape[0]
    width = hidden.shape[1]
    reqs = lax.axis_size("req")
    vocs = lax.axis_size("voc")
    position = lax.axis_index("voc")
    core = lax.axis_index("req") % 2
    start = bounds[0, 0]
    finish = bounds[0, 1]
    live_count = finish - start
    values = hidden.astype(jnp.float32)
    meansq = jnp.mean(values * values, axis=-1, keepdims=True)
    normed_all = (values * lax.rsqrt(meansq + 1e-05) * norm_gain).astype(jnp.bfloat16)
    pick = (
        lax.broadcasted_iota(jnp.int32, (LIVE, slots), 1)
        == lax.broadcasted_iota(jnp.int32, (LIVE, slots), 0) + start
    )
    normed = jnp.dot(pick.astype(jnp.bfloat16), normed_all, preferred_element_type=jnp.float32)
    normed = normed.astype(jnp.bfloat16)
    ids = jnp.dot(
        pick.astype(jnp.float32), targets.astype(jnp.float32), precision=lax.Precision.HIGHEST
    ).astype(jnp.int32)
    column = lax.broadcasted_iota(jnp.int32, (LIVE, EXTRA), 1)
    meta = jnp.where(column == 0, ids[:, None] // 256, ids[:, None] % 256)
    meta = jnp.where(column == 2, live_count, jnp.where(column < 2, meta, 0))
    own = jnp.concatenate([normed, meta.astype(jnp.bfloat16)], axis=1)

    stats = lambda block: block_stats(block, head, position)
    left = shift(own, 0, 1, reqs, vocs)
    right = shift(own, 0, -1, reqs, vocs)
    far = shift(own, 0, 2, reqs, vocs)
    part_near = stats(jnp.concatenate([own, left, right]))
    line = jnp.stack([own, left, right, far])
    halves = lambda step: jnp.concatenate(
        [shift(line[:, :HALF], 1, step, reqs, vocs), shift(line[:, HALF:], 1, step, reqs, vocs)], axis=1
    )
    line_left = halves(1)
    line_right = halves(-1)
    part_far = stats(far)
    line_far = halves(2)
    part_lines = stats(jnp.concatenate([line_left, line_right]).reshape(-1, own.shape[1]))
    part_line_far = stats(line_far.reshape(-1, own.shape[1]))
    processed = jnp.concatenate([part_near, part_far, part_lines, part_line_far], axis=1)
    processed = processed.reshape(4, vocs, LIVE)
    count_of = lambda block: block[..., :1, width + 2].reshape(-1).astype(jnp.int32)
    processed_counts = jnp.concatenate(
        [count_of(line), count_of(line_left), count_of(line_right), count_of(line_far)]
    )

    source = jnp.arange(vocs, dtype=jnp.int32)
    slot_of = jnp.array([0, 2, 3, 1], jnp.int32)
    my_a = jnp.where(core == 0, position % SIDE, position // SIDE)
    my_b = jnp.where(core == 0, position // SIDE, position % SIDE)
    src_a = jnp.where(core == 0, source % SIDE, source // SIDE)
    src_b = jnp.where(core == 0, source // SIDE, source % SIDE)
    where_is = slot_of[(src_b - my_b) % SIDE] * SIDE + slot_of[(src_a - my_a) % SIDE]
    canonical = jnp.take(processed, where_is, axis=1).reshape(4, vocs * LIVE)
    counts = jnp.take(processed_counts, where_is, axis=0)

    merged = butterfly(canonical, "voc", combine_stats, (1, 3, 4, 12))
    top, total, weighted, picked = merged[0], merged[1], merged[2], merged[3]
    lse = top + jnp.log(total)
    row_entropy = lse - weighted / total
    row_logprob = picked - lse
    slot = jnp.arange(LIVE, dtype=jnp.int32)
    group_live = slot[None, :] < counts[:, None]
    group_entropy = jnp.where(group_live, row_entropy.reshape(vocs, LIVE), 0.0)
    totals = jnp.stack([jnp.sum(group_entropy), jnp.sum(counts).astype(jnp.float32)])
    totals = butterfly(totals, "req", lambda a, b: a + b, (1, 2, 6))
    mean_entropy = (totals[0] / totals[1]).reshape(1)
    mine = lambda a: lax.dynamic_slice_in_dim(a, position * LIVE, LIVE, 0)
    live = slot < live_count
    zero = jnp.zeros((LIVE,), jnp.float32)
    place = lambda a: jnp.dot(a, pick.astype(jnp.float32), precision=lax.Precision.HIGHEST)
    entropy = place(jnp.where(live, mine(row_entropy), zero))
    logprob = place(jnp.where(live, mine(row_logprob), zero))
    target_logit = place(jnp.where(live, mine(picked), zero))
    return (logprob, entropy, target_logit, mean_entropy)


def solution(mesh):
    placed = (
        P(AXES, None),
        P(),
        P(None, "voc"),
        P(AXES),
        P(AXES, None),
    )
    return jax.shard_map(
        shards,
        mesh=mesh,
        in_specs=placed,
        out_specs=(P(AXES), P(AXES), P(AXES), P()),
        check_vma=False,
    )
```
